256 devices in a mesh: dp: 16 (over z_lo, x), seq: 16 (over y, z_hi, core).
Axes of the slice: x: 4, y: 4, z: 8 (z_hi: 2, z_lo: 4; z = z_hi * 4 + z_lo), core: 2. Of those that a mesh axis runs over, the one named last changes fastest.
Arguments:
- codes: int32 [16, 32768], P('dp', 'seq'), may hold values from 0 to 3
- embed: bfloat16 [4, 256], replicated, may hold values from -6 to 6
- first_weight_taps: bfloat16 [3, 256, 256], replicated, may hold values from -0.21875 to 0.21875
- second_weight_taps: bfloat16 [3, 256, 256], replicated, may hold values from -0.21875 to 0.21875
- cotangent: bfloat16 [16, 32768, 256], P('dp', 'seq'), may hold values from -6 to 6
Outputs:
- block_out: bfloat16 [16, 32768, 256], P('dp', 'seq')
- first_weight_gradient: float32 [3, 256, 256], replicated
- second_weight_gradient: float32 [3, 256, 256], replicated
The draws below stay inside these ranges and needn't reach their ends.
All inputs are finite; a program needn't handle non-finite values.
Results may differ from the reference program's by a relative error of at most 0.0085.
Values may be sent and summed in bfloat16 or wider, within the bound.
No kernel may reach another device: no remote copies, remote signals or barrier semaphores. Data moves between devices by JAX's collectives and lax.ppermute only.
A program may use at most 64 MiB of HBM per device.

```python
import math
import jax
import jax.numpy as jnp
from jax import lax

CHANNELS = 256
FIRST_DILATION = 4
SECOND_DILATION = 16
SEQLEN = 32768
WINDOWS = 16


def draw_cotangent(key, part):
    edge_rows = 32
    inner_scale = math.sqrt(2.0 * edge_rows / (SEQLEN - 2 * edge_rows))
    position = jnp.arange(SEQLEN, dtype=jnp.int32)
    at_edge = (position < edge_rows) | (position >= SEQLEN - edge_rows)
    envelope = jnp.where(at_edge, jnp.float32(1.0), jnp.float32(inner_scale)).astype(jnp.float32)
    extent = (WINDOWS, SEQLEN, CHANNELS)
    values = jnp.clip(jax.random.normal(key, extent, jnp.float32), -6.0, 6.0)
    return (values * envelope[None, :, None]).astype(jnp.bfloat16)


def with_ends(result, own_key, smallest, largest):
    place = [jax.random.randint(jax.random.fold_in(own_key, axis), (), 0, length) for axis, length in enumerate(result.shape)]
    main_axis = result.shape.index(max(result.shape))
    next_to = place[:main_axis] + [(place[main_axis] + 1) % result.shape[main_axis]] + place[main_axis + 1:]
    return result.at[tuple(place)].set(smallest).at[tuple(next_to)].set(largest)


def noise(rng, shape, deviation, reach, kind=jnp.bfloat16):
    entries = jax.random.normal(rng, shape, jnp.float32) * deviation
    return jnp.minimum(jnp.maximum(entries, -reach), reach).astype(kind)


def setup_inputs(seed: int = 0) -> dict:
    keys = jax.random.split(jax.random.key(seed), 6)
    return {
        "codes": with_ends(jax.random.randint(keys[0], (WINDOWS, SEQLEN), 0, 4), jax.random.fold_in(keys[0], 1), 0, 3).astype(jnp.int32),
        "embed": noise(keys[1], (4, CHANNELS), 1.0, 6.0),
        "first_weight_taps": noise(keys[2], (3, CHANNELS, CHANNELS), (3 * CHANNELS) ** -0.5, 0.21875),
        "second_weight_taps": noise(keys[3], (3, CHANNELS, CHANNELS), (3 * CHANNELS) ** -0.5, 0.21875),
        "cotangent": draw_cotangent(jax.random.fold_in(keys[5], 71), 0),
    }


def strand_flip(value):
    return value[::-1, ::-1]

def stack_shifts(value, dilation, order):
    count_rows = value.shape[0]
    padded = jnp.pad(value, ((dilation, dilation), (0, 0)))
    return jnp.concatenate([padded[k * dilation:k * dilation + count_rows] for k in order], axis=-1)

def dilated_filter(value, weight, dilation):
    flat = weight.reshape(-1, weight.shape[2])
    return jnp.dot(stack_shifts(value, dilation, (0, 1, 2)), flat, preferred_element_type=jnp.float32)

def transposed_filter(grad, weight, dilation):
    flat = jnp.transpose(weight, (0, 2, 1)).reshape(-1, weight.shape[2])
    return jnp.dot(stack_shifts(grad, dilation, (2, 1, 0)), flat, preferred_element_type=jnp.float32)

def weight_gradient_total(value, grad, dilation):
    stacked = stack_shifts(value, dilation, (0, 1, 2))
    term = jnp.dot(stacked.T, grad, preferred_element_type=jnp.float32)
    return term.reshape(3, value.shape[1], value.shape[1])

def one_window(codes_row, cot_row, embed, first_weight_taps, second_weight_taps):
    onehot = (codes_row[:, None] == jnp.arange(4, dtype=jnp.int32)[None, :]).astype(jnp.bfloat16)
    nucleotide_features = jnp.dot(onehot, embed, preferred_element_type=jnp.float32).astype(jnp.bfloat16)
    first_activation = dilated_filter(nucleotide_features, first_weight_taps, FIRST_DILATION) + strand_flip(dilated_filter(strand_flip(nucleotide_features), first_weight_taps, FIRST_DILATION))
    gelu_one, back_one = jax.vjp(jax.nn.gelu, first_activation)
    hidden_state = gelu_one.astype(jnp.bfloat16)
    second_activation = dilated_filter(hidden_state, second_weight_taps, SECOND_DILATION) + strand_flip(dilated_filter(strand_flip(hidden_state), second_weight_taps, SECOND_DILATION))
    gelu_two, back_two = jax.vjp(jax.nn.gelu, second_activation)
    block_out = (hidden_state.astype(jnp.float32) + gelu_two).astype(jnp.bfloat16)
    cotangent_wide_float = cot_row.astype(jnp.float32)
    second_activation_gradient = back_two(cotangent_wide_float)[0].astype(jnp.bfloat16)
    hidden_gradient = cotangent_wide_float + transposed_filter(second_activation_gradient, second_weight_taps, SECOND_DILATION) + strand_flip(transposed_filter(strand_flip(second_activation_gradient), second_weight_taps, SECOND_DILATION))
    first_activation_gradient = back_one(hidden_gradient)[0].astype(jnp.bfloat16)
    second_weight_gradient = weight_gradient_total(hidden_state, second_activation_gradient, SECOND_DILATION) + weight_gradient_total(strand_flip(hidden_state), strand_flip(second_activation_gradient), SECOND_DILATION)
    first_weight_gradient = weight_gradient_total(nucleotide_features, first_activation_gradient, FIRST_DILATION) + weight_gradient_total(strand_flip(nucleotide_features), strand_flip(first_activation_gradient), FIRST_DILATION)
    return (block_out, first_weight_gradient, second_weight_gradient)

def reference(codes, embed, first_weight_taps, second_weight_taps, cotangent):

    def step(pair):
        return one_window(pair[0], pair[1], embed, first_weight_taps, second_weight_taps)
    block_out, first_weight_gradient, second_weight_gradient = lax.map(step, (codes, cotangent))
    return (block_out, lax.optimization_barrier(jnp.sum(first_weight_gradient, axis=0)), lax.optimization_barrier(jnp.sum(second_weight_gradient, axis=0)))
```

```python
import jax
import jax.numpy as jnp
from jax import lax
from jax.sharding import PartitionSpec as P

FIRST_DILATION = 4
SECOND_DILATION = 16


def with_halo(cells, sides, width):
    for axis, dim in sides:
        count = lax.axis_size(axis)
        ends = count - 1
        head = lax.slice_in_dim(cells, 0, width, axis=dim)
        tail = lax.slice_in_dim(cells, cells.shape[dim] - width, cells.shape[dim], axis=dim)
        cells = jnp.concatenate(
            [
                lax.ppermute(tail, axis, [(i, (i + 1) % count) for i in range(ends)]),
                cells,
                lax.ppermute(head, axis, [((i + 1) % count, i) for i in range(ends)]),
            ],
            axis=dim,
        )
    return cells


def pad_rows(value, dilation):
    return with_halo(value, (("seq", 1),), dilation)


def stack_rows(padded, dilation, order):
    count_rows = padded.shape[1] - 2 * dilation
    return jnp.concatenate(
        [padded[:, k * dilation : k * dilation + count_rows] for k in order], axis=-1
    )


def product(stacked, matrix):
    shape_in = stacked.shape
    result = jnp.dot(stacked.reshape(-1, shape_in[-1]), matrix, preferred_element_type=jnp.float32)
    return result.reshape(shape_in[:-1] + (matrix.shape[1],))


def weight_term(stacked, grad):
    channels = grad.shape[-1]
    term = jnp.dot(
        stacked.reshape(-1, 3 * channels).T,
        grad.reshape(-1, channels),
        preferred_element_type=jnp.float32,
    )
    return term.reshape(3, channels, channels)


def layer_forward_pass(value, weight, dilation):
    channels = weight.shape[2]
    stacked = stack_rows(pad_rows(value, dilation), dilation, (0, 1, 2))
    flat = weight.reshape(-1, channels)
    reversed_taps = weight[::-1, ::-1, ::-1].reshape(-1, channels)
    both = product(stacked, jnp.concatenate([flat, reversed_taps], axis=1))
    return (both[..., :channels] + both[..., channels:], stacked)


def input_backward_pass(grad, weight, dilation):
    channels = weight.shape[2]
    stacked = stack_rows(pad_rows(grad, dilation), dilation, (2, 1, 0))
    flat_t = jnp.transpose(weight, (0, 2, 1)).reshape(-1, channels)
    reversed_t = jnp.transpose(weight[::-1, ::-1, ::-1], (0, 2, 1)).reshape(-1, channels)
    both = product(stacked, jnp.concatenate([flat_t, reversed_t], axis=1))
    return both[..., :channels] + both[..., channels:]


def strand_total(stacked, grad):
    term = weight_term(stacked, grad)
    return term + term[::-1, ::-1, ::-1]


def exchange_steps():
    steps = []
    for axis, bit in (("seq", 1), ("dp", 1), ("dp", 2), ("seq", 4), ("seq", 8), ("dp", 4), ("dp", 8), ("seq", 2)):
        if bit < lax.axis_size(axis):
            steps.append((axis, bit))
    return steps


def butterfly_sum(rows):
    kept = []
    for axis, bit in exchange_steps():
        count = lax.axis_size(axis)
        pairs = [(i, i ^ bit) for i in range(count)]
        half = rows.shape[0] // 2
        upper = (lax.axis_index(axis) & bit) != 0
        low, high = rows[:half], rows[half:]
        mine = jnp.where(upper, high, low)
        other = jnp.where(upper, low, high)
        rows = mine + lax.ppermute(other, axis, pairs)
        kept.append((axis, bit, upper))
    for axis, bit, upper in reversed(kept):
        count = lax.axis_size(axis)
        pairs = [(i, i ^ bit) for i in range(count)]
        got = lax.ppermute(rows, axis, pairs)
        rows = jnp.where(upper, jnp.concatenate([got, rows]), jnp.concatenate([rows, got]))
    return rows


def symmetric_sum(first, second):
    shape = first.shape
    flat_rows = shape[0] * shape[1]
    half = flat_rows // 2
    halves = [g.reshape(flat_rows, shape[2])[:half] for g in (first, second)]
    total = butterfly_sum(jnp.concatenate(halves, axis=0))
    outs = []
    for i in range(2):
        part = total[i * half : (i + 1) * half]
        outs.append(jnp.concatenate([part, part[::-1, ::-1]], axis=0).reshape(shape))
    return outs


def local(codes, embed, first_weight_taps, second_weight_taps, cotangent):
    onehot = (codes[..., None] == jnp.arange(4, dtype=jnp.int32)).astype(jnp.bfloat16)
    nucleotide_features = product(onehot, embed).astype(jnp.bfloat16)
    first_activation, first_shift_stack = layer_forward_pass(
        nucleotide_features, first_weight_taps, FIRST_DILATION
    )
    gelu_one, back_one = jax.vjp(jax.nn.gelu, first_activation)
    hidden_state = gelu_one.astype(jnp.bfloat16)
    second_activation, second_shift_stack = layer_forward_pass(
        hidden_state, second_weight_taps, SECOND_DILATION
    )
    gelu_two, back_two = jax.vjp(jax.nn.gelu, second_activation)
    block_out = (hidden_state.astype(jnp.float32) + gelu_two).astype(jnp.bfloat16)
    cotangent_wide_float = cotangent.astype(jnp.float32)
    second_activation_gradient = back_two(cotangent_wide_float)[0].astype(jnp.bfloat16)
    input_contribution = input_backward_pass(
        second_activation_gradient, second_weight_taps, SECOND_DILATION
    )
    second_weight_gradient = strand_total(second_shift_stack, second_activation_gradient)
    hidden_gradient = cotangent_wide_float + input_contribution
    first_activation_gradient = back_one(hidden_gradient)[0].astype(jnp.bfloat16)
    first_weight_gradient = strand_total(first_shift_stack, first_activation_gradient)
    second_weight_gradient, first_weight_gradient = symmetric_sum(
        second_weight_gradient, first_weight_gradient
    )
    return (block_out, first_weight_gradient, second_weight_gradient)


def solution(mesh):
    in_specs = (P("dp", "seq"), P(), P(), P(), P("dp", "seq", None))
    out_specs = (P("dp", "seq", None), P(), P())
    return jax.shard_map(local, mesh=mesh, in_specs=in_specs, out_specs=out_specs, check_vma=False)
```

```python
import jax
import jax.numpy as jnp
from jax import lax
from jax.sharding import PartitionSpec as P

FIRST_DILATION = 4
SECOND_DILATION = 16


def with_halo(cells, sides, width):
    for axis, dim in sides:
        count = lax.axis_size(axis)
        ends = count - 1
        head = lax.slice_in_dim(cells, 0, width, axis=dim)
        tail = lax.slice_in_dim(cells, cells.shape[dim] - width, cells.shape[dim], axis=dim)
        cells = jnp.concatenate(
            [
                lax.ppermute(tail, axis, [(i, (i + 1) % count) for i in range(ends)]),
                cells,
                lax.ppermute(head, axis, [((i + 1) % count, i) for i in range(ends)]),
            ],
            axis=dim,
        )
    return cells


def pad_rows(value, dilation):
    return with_halo(value, (("seq", 1),), dilation)


def stack_rows(padded, dilation, order):
    count_rows = padded.shape[1] - 2 * dilation
    return jnp.concatenate(
        [padded[:, k * dilation : k * dilation + count_rows] for k in order], axis=-1
    )


def product(stacked, matrix):
    shape_in = stacked.shape
    result = jnp.dot(stacked.reshape(-1, shape_in[-1]), matrix, preferred_element_type=jnp.float32)
    return result.reshape(shape_in[:-1] + (matrix.shape[1],))


def weight_term(stacked, grad):
    channels = grad.shape[-1]
    term = jnp.dot(
        stacked.reshape(-1, 3 * channels).T,
        grad.reshape(-1, channels),
        preferred_element_type=jnp.float32,
    )
    return term.reshape(3, channels, channels)


def layer_forward_pass(value, weight, dilation):
    channels = weight.shape[2]
    stacked = stack_rows(pad_rows(value, dilation), dilation, (0, 1, 2))
    flat = weight.reshape(-1, channels)
    reversed_taps = weight[::-1, ::-1, ::-1].reshape(-1, channels)
    both = product(stacked, jnp.concatenate([flat, reversed_taps], axis=1))
    return (both[..., :channels] + both[..., channels:], stacked)


def input_backward_pass(grad, weight, dilation):
    channels = weight.shape[2]
    stacked = stack_rows(pad_rows(grad, dilation), dilation, (2, 1, 0))
    flat_t = jnp.transpose(weight, (0, 2, 1)).reshape(-1, channels)
    reversed_t = jnp.transpose(weight[::-1, ::-1, ::-1], (0, 2, 1)).reshape(-1, channels)
    both = product(stacked, jnp.concatenate([flat_t, reversed_t], axis=1))
    return both[..., :channels] + both[..., channels:]


def strand_total(stacked, grad):
    term = weight_term(stacked, grad)
    return term + term[::-1, ::-1, ::-1]


def exchange_groups():
    groups = []
    for axis, shift, radix in (("dp", 0, 4), ("seq", 2, 4), ("dp", 2, 4), ("seq", 0, 4)):
        if (radix << shift) <= lax.axis_size(axis):
            groups.append((axis, shift, radix))
    return groups


def partner_pairs(axis, shift, offset):
    count = lax.axis_size(axis)
    return [(i, i ^ (offset << shift)) for i in range(count)]


def butterfly_sum(rows):
    kept = []
    for axis, shift, radix in exchange_groups():
        place = (lax.axis_index(axis) >> shift) & (radix - 1)
        width = rows.shape[0] // radix
        total = lax.dynamic_slice_in_dim(rows, place * width, width)
        for offset in range(1, radix):
            sent = lax.dynamic_slice_in_dim(rows, (place ^ offset) * width, width)
            total = total + lax.ppermute(sent, axis, partner_pairs(axis, shift, offset))
        rows = total
        kept.append((axis, shift, radix, place))
    for axis, shift, radix, place in reversed(kept):
        width = rows.shape[0]
        full = jnp.zeros((width * radix,) + rows.shape[1:], rows.dtype)
        full = lax.dynamic_update_slice_in_dim(full, rows, place * width, 0)
        for offset in range(1, radix):
            got = lax.ppermute(rows, axis, partner_pairs(axis, shift, offset))
            full = lax.dynamic_update_slice_in_dim(full, got, (place ^ offset) * width, 0)
        rows = full
    return rows


def symmetric_sum(first, second):
    shape = first.shape
    flat_rows = shape[0] * shape[1]
    half = flat_rows // 2
    halves = [g.reshape(flat_rows, shape[2])[:half] for g in (first, second)]
    total = butterfly_sum(jnp.concatenate(halves, axis=0))
    outs = []
    for i in range(2):
        part = total[i * half : (i + 1) * half]
        outs.append(jnp.concatenate([part, part[::-1, ::-1]], axis=0).reshape(shape))
    return outs


def local(codes, embed, first_weight_taps, second_weight_taps, cotangent):
    onehot = (codes[..., None] == jnp.arange(4, dtype=jnp.int32)).astype(jnp.bfloat16)
    nucleotide_features = product(onehot, embed).astype(jnp.bfloat16)
    first_activation, first_shift_stack = layer_forward_pass(
        nucleotide_features, first_weight_taps, FIRST_DILATION
    )
    gelu_one, back_one = jax.vjp(jax.nn.gelu, first_activation)
    hidden_state = gelu_one.astype(jnp.bfloat16)
    second_activation, second_shift_stack = layer_forward_pass(
        hidden_state, second_weight_taps, SECOND_DILATION
    )
    gelu_two, back_two = jax.vjp(jax.nn.gelu, second_activation)
    block_out = (hidden_state.astype(jnp.float32) + gelu_two).astype(jnp.bfloat16)
    cotangent_wide_float = cotangent.astype(jnp.float32)
    second_activation_gradient = back_two(cotangent_wide_float)[0].astype(jnp.bfloat16)
    input_contribution = input_backward_pass(
        second_activation_gradient, second_weight_taps, SECOND_DILATION
    )
    second_weight_gradient = strand_total(second_shift_stack, second_activation_gradient)
    hidden_gradient = cotangent_wide_float + input_contribution
    first_activation_gradient = back_one(hidden_gradient)[0].astype(jnp.bfloat16)
    first_weight_gradient = strand_total(first_shift_stack, first_activation_gradient)
    second_weight_gradient, first_weight_gradient = symmetric_sum(
        second_weight_gradient, first_weight_gradient
    )
    return (block_out, first_weight_gradient, second_weight_gradient)


def solution(mesh):
    in_specs = (P("dp", "seq"), P(), P(), P(), P("dp", "seq", None))
    out_specs = (P("dp", "seq", None), P(), P())
    return jax.shard_map(local, mesh=mesh, in_specs=in_specs, out_specs=out_specs, check_vma=False)
```

```python
import jax
import jax.numpy as jnp
from jax import lax
from jax.sharding import PartitionSpec as P

FIRST_DILATION = 4
SECOND_DILATION = 16


def with_halo(cells, sides, width):
    for axis, dim in sides:
        count = lax.axis_size(axis)
        ends = count - 1
        head = lax.slice_in_dim(cells, 0, width, axis=dim)
        tail = lax.slice_in_dim(cells, cells.shape[dim] - width, cells.shape[dim], axis=dim)
        cells = jnp.concatenate(
            [
                lax.ppermute(tail, axis, [(i, (i + 1) % count) for i in range(ends)]),
                cells,
                lax.ppermute(head, axis, [((i + 1) % count, i) for i in range(ends)]),
            ],
            axis=dim,
        )
    return cells


def pad_rows(value, dilation):
    return with_halo(value, (("seq", 1),), dilation)


def stack_rows(padded, dilation, order):
    count_rows = padded.shape[1] - 2 * dilation
    return jnp.concatenate(
        [padded[:, k * dilation : k * dilation + count_rows] for k in order], axis=-1
    )


def product(stacked, matrix):
    shape_in = stacked.shape
    result = jnp.dot(stacked.reshape(-1, shape_in[-1]), matrix, preferred_element_type=jnp.float32)
    return result.reshape(shape_in[:-1] + (matrix.shape[1],))


def weight_term(stacked, grad):
    channels = grad.shape[-1]
    term = jnp.dot(
        stacked.reshape(-1, 3 * channels).T,
        grad.reshape(-1, channels),
        preferred_element_type=jnp.float32,
    )
    return term.reshape(3, channels, channels)


def layer_forward_pass(value, weight, dilation):
    channels = weight.shape[2]
    stacked = stack_rows(pad_rows(value, dilation), dilation, (0, 1, 2))
    flat = weight.reshape(-1, channels)
    reversed_taps = weight[::-1, ::-1, ::-1].reshape(-1, channels)
    both = product(stacked, jnp.concatenate([flat, reversed_taps], axis=1))
    return (both[..., :channels] + both[..., channels:], stacked)


def input_backward_pass(grad, weight, dilation):
    channels = weight.shape[2]
    stacked = stack_rows(pad_rows(grad, dilation), dilation, (2, 1, 0))
    flat_t = jnp.transpose(weight, (0, 2, 1)).reshape(-1, channels)
    reversed_t = jnp.transpose(weight[::-1, ::-1, ::-1], (0, 2, 1)).reshape(-1, channels)
    both = product(stacked, jnp.concatenate([flat_t, reversed_t], axis=1))
    return both[..., :channels] + both[..., channels:]


def strand_total(stacked, grad):
    term = weight_term(stacked, grad)
    return term + term[::-1, ::-1, ::-1]


def exchange_groups():
    groups = []
    for axis, shift, radix in (("dp", 0, 4), ("seq", 2, 4), ("dp", 2, 4), ("seq", 0, 4)):
        if (radix << shift) <= lax.axis_size(axis):
            groups.append((axis, shift, radix))
    return groups


def partner_pairs(axis, shift, offset):
    count = lax.axis_size(axis)
    return [(i, i ^ (offset << shift)) for i in range(count)]


def butterfly_sum(rows):
    kept = []
    for axis, shift, radix in exchange_groups():
        place = (lax.axis_index(axis) >> shift) & (radix - 1)
        width = rows.shape[0] // radix
        total = lax.dynamic_slice_in_dim(rows, place * width, width)
        for offset in range(1, radix):
            sent = lax.dynamic_slice_in_dim(rows, (place ^ offset) * width, width)
            total = total + lax.ppermute(sent, axis, partner_pairs(axis, shift, offset))
        rows = total
        kept.append((axis, shift, radix, place))
    for axis, shift, radix, place in reversed(kept):
        width = rows.shape[0]
        full = jnp.zeros((width * radix,) + rows.shape[1:], rows.dtype)
        full = lax.dynamic_update_slice_in_dim(full, rows, place * width, 0)
        for offset in range(1, radix):
            got = lax.ppermute(rows, axis, partner_pairs(axis, shift, offset))
            full = lax.dynamic_update_slice_in_dim(full, got, (place ^ offset) * width, 0)
        rows = full
    return rows


def symmetric_sum(first, second):
    shape = first.shape
    flat_rows = shape[0] * shape[1]
    half = flat_rows // 2
    halves = [g.reshape(flat_rows, shape[2])[:half] for g in (first, second)]
    total = butterfly_sum(jnp.concatenate(halves, axis=0))
    outs = []
    for i in range(2):
        part = total[i * half : (i + 1) * half]
        outs.append(jnp.concatenate([part, part[::-1, ::-1]], axis=0).reshape(shape))
    return outs


def neighbour_halo(cells, width, dim):
    count = lax.axis_size("seq")
    head = lax.slice_in_dim(cells, 0, width, axis=dim)
    tail = lax.slice_in_dim(cells, cells.shape[dim] - width, cells.shape[dim], axis=dim)
    from_left = lax.ppermute(tail, "seq", [(i, i + 1) for i in range(count - 1)])
    from_right = lax.ppermute(head, "seq", [(i + 1, i) for i in range(count - 1)])
    return from_left, from_right


def inside_window(rows, reach):
    panel = rows - 2 * reach
    place = lax.axis_index("seq") * panel + jnp.arange(rows, dtype=jnp.int32) - reach
    return (place >= 0) & (place < lax.axis_size("seq") * panel)


def anti_diagonal(channels):
    i = jnp.arange(channels, dtype=jnp.int32)
    return (i[:, None] + i[None, :] == channels - 1).astype(jnp.bfloat16)


def mirrored_taps(weight):
    anti = anti_diagonal(weight.shape[1])
    flipped = weight[::-1]
    left = jnp.einsum("ab,kbc->kac", anti, flipped, preferred_element_type=jnp.float32).astype(weight.dtype)
    return jnp.einsum("kab,bc->kac", left, anti, preferred_element_type=jnp.float32).astype(weight.dtype)


def both_strands(stacked, matrix, mirrored):
    channels = matrix.shape[2]
    both = product(stacked, jnp.concatenate([matrix.reshape(-1, channels), mirrored.reshape(-1, channels)], axis=1))
    return both[..., :channels] + both[..., channels:]


def taps_of(padded, dilation, rows, order):
    return jnp.concatenate(
        [lax.slice_in_dim(padded, k * dilation, k * dilation + rows, axis=1) for k in order], axis=-1
    )


def local(codes, embed, first_weight_taps, second_weight_taps, cotangent):
    one, two = FIRST_DILATION, SECOND_DILATION
    panel = codes.shape[1]
    reach_hidden = 2 * two
    reach_codes = reach_hidden + one
    code_left, code_right = neighbour_halo(codes, reach_codes, 1)
    cot_left, cot_right = neighbour_halo(cotangent, two, 1)
    codes_wide = jnp.concatenate([code_left, codes, code_right], axis=1)
    cot_wide = jnp.concatenate([cot_left, cotangent, cot_right], axis=1)

    first_mirror = mirrored_taps(first_weight_taps)
    second_mirror = mirrored_taps(second_weight_taps)

    onehot = (codes_wide[..., None] == jnp.arange(4, dtype=jnp.int32)).astype(jnp.bfloat16)
    features = product(onehot, embed).astype(jnp.bfloat16)
    rows_codes = panel + 2 * reach_codes
    features = jnp.where(inside_window(rows_codes, reach_codes)[None, :, None], features, jnp.zeros_like(features))

    rows_hidden = panel + 2 * reach_hidden
    first_stack = taps_of(features, one, rows_hidden, (0, 1, 2))
    first_activation = both_strands(first_stack, first_weight_taps, first_mirror)
    hidden = jax.nn.gelu(first_activation).astype(jnp.bfloat16)
    hidden = jnp.where(inside_window(rows_hidden, reach_hidden)[None, :, None], hidden, jnp.zeros_like(hidden))

    rows_two = panel + 2 * two
    second_stack = taps_of(hidden, two, rows_two, (0, 1, 2))
    second_activation = both_strands(second_stack, second_weight_taps, second_mirror)
    gelu_two, back_two = jax.vjp(jax.nn.gelu, second_activation)

    hidden_own = lax.slice_in_dim(hidden, reach_hidden, reach_hidden + panel, axis=1)
    block_out = (hidden_own.astype(jnp.float32) + lax.slice_in_dim(gelu_two, two, two + panel, axis=1)).astype(jnp.bfloat16)

    second_grad_wide = back_two(cot_wide.astype(jnp.float32))[0].astype(jnp.bfloat16)
    grad_stack = taps_of(second_grad_wide, two, panel, (2, 1, 0))
    flat_t = jnp.transpose(second_weight_taps, (0, 2, 1))
    mirror_t = jnp.transpose(second_mirror, (0, 2, 1))
    input_contribution = both_strands(grad_stack, flat_t, mirror_t)
    hidden_gradient = cotangent.astype(jnp.float32) + input_contribution

    first_own = lax.slice_in_dim(first_activation, reach_hidden, reach_hidden + panel, axis=1)
    _, back_one = jax.vjp(jax.nn.gelu, first_own)
    first_grad = back_one(hidden_gradient)[0].astype(jnp.bfloat16)

    second_grad_own = lax.slice_in_dim(second_grad_wide, two, two + panel, axis=1)
    second_weight_gradient = strand_total(lax.slice_in_dim(second_stack, two, two + panel, axis=1), second_grad_own)
    first_weight_gradient = strand_total(
        lax.slice_in_dim(first_stack, reach_hidden, reach_hidden + panel, axis=1), first_grad
    )
    second_weight_gradient, first_weight_gradient = symmetric_sum(second_weight_gradient, first_weight_gradient)
    return (block_out, first_weight_gradient, second_weight_gradient)


def solution(mesh):
    in_specs = (P("dp", "seq"), P(), P(), P(), P("dp", "seq", None))
    out_specs = (P("dp", "seq", None), P(), P())
    return jax.shard_map(local, mesh=mesh, in_specs=in_specs, out_specs=out_specs, check_vma=False)
```

```python
import jax
import jax.numpy as jnp
from jax import lax
from jax.sharding import PartitionSpec as P

FIRST_DILATION = 4
SECOND_DILATION = 16


def with_halo(cells, sides, width):
    for axis, dim in sides:
        count = lax.axis_size(axis)
        ends = count - 1
        head = lax.slice_in_dim(cells, 0, width, axis=dim)
        tail = lax.slice_in_dim(cells, cells.shape[dim] - width, cells.shape[dim], axis=dim)
        cells = jnp.concatenate(
            [
                lax.ppermute(tail, axis, [(i, (i + 1) % count) for i in range(ends)]),
                cells,
                lax.ppermute(head, axis, [((i + 1) % count, i) for i in range(ends)]),
            ],
            axis=dim,
        )
    return cells


def pad_rows(value, dilation):
    return with_halo(value, (("seq", 1),), dilation)


def stack_rows(padded, dilation, order):
    count_rows = padded.shape[1] - 2 * dilation
    return jnp.concatenate(
        [padded[:, k * dilation : k * dilation + count_rows] for k in order], axis=-1
    )


def product(stacked, matrix):
    shape_in = stacked.shape
    result = jnp.dot(stacked.reshape(-1, shape_in[-1]), matrix, preferred_element_type=jnp.float32)
    return result.reshape(shape_in[:-1] + (matrix.shape[1],))


def weight_term(stacked, grad):
    channels = grad.shape[-1]
    term = jnp.dot(
        stacked.reshape(-1, 3 * channels).T,
        grad.reshape(-1, channels),
        preferred_element_type=jnp.float32,
    )
    return term.reshape(3, channels, channels)


def layer_forward_pass(value, weight, dilation):
    channels = weight.shape[2]
    stacked = stack_rows(pad_rows(value, dilation), dilation, (0, 1, 2))
    flat = weight.reshape(-1, channels)
    reversed_taps = weight[::-1, ::-1, ::-1].reshape(-1, channels)
    both = product(stacked, jnp.concatenate([flat, reversed_taps], axis=1))
    return (both[..., :channels] + both[..., channels:], stacked)


def input_backward_pass(grad, weight, dilation):
    channels = weight.shape[2]
    stacked = stack_rows(pad_rows(grad, dilation), dilation, (2, 1, 0))
    flat_t = jnp.transpose(weight, (0, 2, 1)).reshape(-1, channels)
    reversed_t = jnp.transpose(weight[::-1, ::-1, ::-1], (0, 2, 1)).reshape(-1, channels)
    both = product(stacked, jnp.concatenate([flat_t, reversed_t], axis=1))
    return both[..., :channels] + both[..., channels:]


def strand_total(stacked, grad):
    term = weight_term(stacked, grad)
    return term + term[::-1, ::-1, ::-1]


def exchange_groups():
    groups = []
    for axis, shift, radix in (("dp", 0, 4), ("seq", 2, 4), ("dp", 2, 4), ("seq", 0, 4)):
        if (radix << shift) <= lax.axis_size(axis):
            groups.append((axis, shift, radix))
    return groups


def partner_pairs(axis, shift, offset):
    count = lax.axis_size(axis)
    return [(i, i ^ (offset << shift)) for i in range(count)]


def butterfly_sum(rows):
    kept = []
    for axis, shift, radix in exchange_groups():
        place = (lax.axis_index(axis) >> shift) & (radix - 1)
        width = rows.shape[0] // radix
        total = lax.dynamic_slice_in_dim(rows, place * width, width)
        for offset in range(1, radix):
            sent = lax.dynamic_slice_in_dim(rows, (place ^ offset) * width, width)
            total = total + lax.ppermute(sent, axis, partner_pairs(axis, shift, offset))
        rows = total
        kept.append((axis, shift, radix, place))
    for axis, shift, radix, place in reversed(kept):
        width = rows.shape[0]
        full = jnp.zeros((width * radix,) + rows.shape[1:], rows.dtype)
        full = lax.dynamic_update_slice_in_dim(full, rows, place * width, 0)
        for offset in range(1, radix):
            got = lax.ppermute(rows, axis, partner_pairs(axis, shift, offset))
            full = lax.dynamic_update_slice_in_dim(full, got, (place ^ offset) * width, 0)
        rows = full
    return rows


def folded_term(stacked, grad):
    channels = grad.shape[-1]
    term = jnp.dot(
        grad.reshape(-1, channels).T,
        stacked.reshape(-1, 3 * channels),
        preferred_element_type=jnp.float32,
    )
    half = channels // 2
    return term[:half] + term[half:][::-1, ::-1]


def unfolded_sums(first, second):
    half, width = first.shape
    total = butterfly_sum(jnp.concatenate([first, second], axis=0))
    outs = []
    for i in range(2):
        part = total[i * half : (i + 1) * half]
        full = jnp.concatenate([part, part[::-1, ::-1]], axis=0)
        outs.append(jnp.transpose(full.reshape(2 * half, 3, width // 3), (1, 2, 0)))
    return outs


def symmetric_sum(first, second):
    shape = first.shape
    flat_rows = shape[0] * shape[1]
    half = flat_rows // 2
    halves = [g.reshape(flat_rows, shape[2])[:half] for g in (first, second)]
    total = butterfly_sum(jnp.concatenate(halves, axis=0))
    outs = []
    for i in range(2):
        part = total[i * half : (i + 1) * half]
        outs.append(jnp.concatenate([part, part[::-1, ::-1]], axis=0).reshape(shape))
    return outs


def neighbour_halo(cells, width, dim):
    count = lax.axis_size("seq")
    head = lax.slice_in_dim(cells, 0, width, axis=dim)
    tail = lax.slice_in_dim(cells, cells.shape[dim] - width, cells.shape[dim], axis=dim)
    from_left = lax.ppermute(tail, "seq", [(i, i + 1) for i in range(count - 1)])
    from_right = lax.ppermute(head, "seq", [(i + 1, i) for i in range(count - 1)])
    return from_left, from_right


def inside_window(rows, reach):
    panel = rows - 2 * reach
    place = lax.axis_index("seq") * panel + jnp.arange(rows, dtype=jnp.int32) - reach
    return (place >= 0) & (place < lax.axis_size("seq") * panel)


def anti_diagonal(channels):
    i = jnp.arange(channels, dtype=jnp.int32)
    return (i[:, None] + i[None, :] == channels - 1).astype(jnp.bfloat16)


def mirrored_taps(weight):
    anti = anti_diagonal(weight.shape[1])
    flipped = weight[::-1]
    left = jnp.einsum("ab,kbc->kac", anti, flipped, preferred_element_type=jnp.float32).astype(weight.dtype)
    return jnp.einsum("kab,bc->kac", left, anti, preferred_element_type=jnp.float32).astype(weight.dtype)


def both_strands(stacked, matrix, mirrored):
    channels = matrix.shape[2]
    both = product(stacked, jnp.concatenate([matrix.reshape(-1, channels), mirrored.reshape(-1, channels)], axis=1))
    return both[..., :channels] + both[..., channels:]


def taps_of(padded, dilation, rows, order):
    return jnp.concatenate(
        [lax.slice_in_dim(padded, k * dilation, k * dilation + rows, axis=1) for k in order], axis=-1
    )


def local(codes, embed, first_weight_taps, second_weight_taps, cotangent):
    one, two = FIRST_DILATION, SECOND_DILATION
    panel = codes.shape[1]
    reach_hidden = 2 * two
    reach_codes = reach_hidden + one
    code_left, code_right = neighbour_halo(codes, reach_codes, 1)
    cot_left, cot_right = neighbour_halo(cotangent, two, 1)
    codes_wide = jnp.concatenate([code_left, codes, code_right], axis=1)
    cot_wide = jnp.concatenate([cot_left, cotangent, cot_right], axis=1)

    first_mirror = mirrored_taps(first_weight_taps)
    second_mirror = mirrored_taps(second_weight_taps)

    onehot = (codes_wide[..., None] == jnp.arange(4, dtype=jnp.int32)).astype(jnp.bfloat16)
    features = product(onehot, embed).astype(jnp.bfloat16)
    rows_codes = panel + 2 * reach_codes
    features = jnp.where(inside_window(rows_codes, reach_codes)[None, :, None], features, jnp.zeros_like(features))

    rows_hidden = panel + 2 * reach_hidden
    first_stack = taps_of(features, one, rows_hidden, (0, 1, 2))
    first_activation = both_strands(first_stack, first_weight_taps, first_mirror)
    hidden = jax.nn.gelu(first_activation).astype(jnp.bfloat16)
    hidden = jnp.where(inside_window(rows_hidden, reach_hidden)[None, :, None], hidden, jnp.zeros_like(hidden))

    rows_two = panel + 2 * two
    second_stack = taps_of(hidden, two, rows_two, (0, 1, 2))
    second_activation = both_strands(second_stack, second_weight_taps, second_mirror)
    gelu_two, back_two = jax.vjp(jax.nn.gelu, second_activation)

    hidden_own = lax.slice_in_dim(hidden, reach_hidden, reach_hidden + panel, axis=1)
    block_out = (hidden_own.astype(jnp.float32) + lax.slice_in_dim(gelu_two, two, two + panel, axis=1)).astype(jnp.bfloat16)

    second_grad_wide = back_two(cot_wide.astype(jnp.float32))[0].astype(jnp.bfloat16)
    grad_stack = taps_of(second_grad_wide, two, panel, (2, 1, 0))
    flat_t = jnp.transpose(second_weight_taps, (0, 2, 1))
    mirror_t = jnp.transpose(second_mirror, (0, 2, 1))
    input_contribution = both_strands(grad_stack, flat_t, mirror_t)
    hidden_gradient = cotangent.astype(jnp.float32) + input_contribution

    first_own = lax.slice_in_dim(first_activation, reach_hidden, reach_hidden + panel, axis=1)
    _, back_one = jax.vjp(jax.nn.gelu, first_own)
    first_grad = back_one(hidden_gradient)[0].astype(jnp.bfloat16)

    second_grad_own = lax.slice_in_dim(second_grad_wide, two, two + panel, axis=1)
    second_weight_gradient = folded_term(lax.slice_in_dim(second_stack, two, two + panel, axis=1), second_grad_own)
    first_weight_gradient = folded_term(
        lax.slice_in_dim(first_stack, reach_hidden, reach_hidden + panel, axis=1), first_grad
    )
    second_weight_gradient, first_weight_gradient = unfolded_sums(second_weight_gradient, first_weight_gradient)
    return (block_out, first_weight_gradient, second_weight_gradient)


def solution(mesh):
    in_specs = (P("dp", "seq"), P(), P(), P(), P("dp", "seq", None))
    out_specs = (P("dp", "seq", None), P(), P())
    return jax.shard_map(local, mesh=mesh, in_specs=in_specs, out_specs=out_specs, check_vma=False)
```

```python
import jax
import jax.numpy as jnp
from jax import lax
from jax.sharding import PartitionSpec as P

FIRST_DILATION = 4
SECOND_DILATION = 16


def with_halo(cells, sides, width):
    for axis, dim in sides:
        count = lax.axis_size(axis)
        ends = count - 1
        head = lax.slice_in_dim(cells, 0, width, axis=dim)
        tail = lax.slice_in_dim(cells, cells.shape[dim] - width, cells.shape[dim], axis=dim)
        cells = jnp.concatenate(
            [
                lax.ppermute(tail, axis, [(i, (i + 1) % count) for i in range(ends)]),
                cells,
                lax.ppermute(head, axis, [((i + 1) % count, i) for i in range(ends)]),
            ],
            axis=dim,
        )
    return cells


def pad_rows(value, dilation):
    return with_halo(value, (("seq", 1),), dilation)


def stack_rows(padded, dilation, order):
    count_rows = padded.shape[1] - 2 * dilation
    return jnp.concatenate(
        [padded[:, k * dilation : k * dilation + count_rows] for k in order], axis=-1
    )


def product(stacked, matrix):
    shape_in = stacked.shape
    result = jnp.dot(stacked.reshape(-1, shape_in[-1]), matrix, preferred_element_type=jnp.float32)
    return result.reshape(shape_in[:-1] + (matrix.shape[1],))


def weight_term(stacked, grad):
    channels = grad.shape[-1]
    term = jnp.dot(
        stacked.reshape(-1, 3 * channels).T,
        grad.reshape(-1, channels),
        preferred_element_type=jnp.float32,
    )
    return term.reshape(3, channels, channels)


def layer_forward_pass(value, weight, dilation):
    channels = weight.shape[2]
    stacked = stack_rows(pad_rows(value, dilation), dilation, (0, 1, 2))
    flat = weight.reshape(-1, channels)
    reversed_taps = weight[::-1, ::-1, ::-1].reshape(-1, channels)
    both = product(stacked, jnp.concatenate([flat, reversed_taps], axis=1))
    return (both[..., :channels] + both[..., channels:], stacked)


def input_backward_pass(grad, weight, dilation):
    channels = weight.shape[2]
    stacked = stack_rows(pad_rows(grad, dilation), dilation, (2, 1, 0))
    flat_t = jnp.transpose(weight, (0, 2, 1)).reshape(-1, channels)
    reversed_t = jnp.transpose(weight[::-1, ::-1, ::-1], (0, 2, 1)).reshape(-1, channels)
    both = product(stacked, jnp.concatenate([flat_t, reversed_t], axis=1))
    return both[..., :channels] + both[..., channels:]


def strand_total(stacked, grad):
    term = weight_term(stacked, grad)
    return term + term[::-1, ::-1, ::-1]


def exchange_groups():
    groups = []
    for axis, shift, radix in (("dp", 0, 4), ("seq", 2, 4), ("dp", 2, 4), ("seq", 0, 4)):
        if (radix << shift) <= lax.axis_size(axis):
            groups.append((axis, shift, radix))
    return groups


def partner_pairs(axis, shift, offset):
    count = lax.axis_size(axis)
    return [(i, i ^ (offset << shift)) for i in range(count)]


def butterfly_sum(rows):
    kept = []
    for axis, shift, radix in exchange_groups():
        place = (lax.axis_index(axis) >> shift) & (radix - 1)
        width = rows.shape[0] // radix
        total = lax.dynamic_slice_in_dim(rows, place * width, width)
        for offset in range(1, radix):
            sent = lax.dynamic_slice_in_dim(rows, (place ^ offset) * width, width)
            total = total + lax.ppermute(sent, axis, partner_pairs(axis, shift, offset))
        rows = total
        kept.append((axis, shift, radix, place))
    for axis, shift, radix, place in reversed(kept):
        width = rows.shape[0]
        full = jnp.zeros((width * radix,) + rows.shape[1:], rows.dtype)
        full = lax.dynamic_update_slice_in_dim(full, rows, place * width, 0)
        for offset in range(1, radix):
            got = lax.ppermute(rows, axis, partner_pairs(axis, shift, offset))
            full = lax.dynamic_update_slice_in_dim(full, got, (place ^ offset) * width, 0)
        rows = full
    return rows


def folded_term(stacked, grad):
    channels = grad.shape[-1]
    term = jnp.dot(
        grad.reshape(-1, channels).T,
        stacked.reshape(-1, 3 * channels),
        preferred_element_type=jnp.float32,
    )
    half = channels // 2
    return term[:half] + term[half:][::-1, ::-1]


def unfolded_sums(first, second):
    half, width = first.shape
    lanes = width // 3
    rows = half * 3
    total = butterfly_sum(jnp.concatenate([first.reshape(rows, lanes), second.reshape(rows, lanes)], axis=0))
    outs = []
    for i in range(2):
        part = total[i * rows : (i + 1) * rows].reshape(half, width)
        full = jnp.concatenate([part, part[::-1, ::-1]], axis=0)
        outs.append(jnp.transpose(full.reshape(2 * half, 3, width // 3), (1, 2, 0)))
    return outs


def symmetric_sum(first, second):
    shape = first.shape
    flat_rows = shape[0] * shape[1]
    half = flat_rows // 2
    halves = [g.reshape(flat_rows, shape[2])[:half] for g in (first, second)]
    total = butterfly_sum(jnp.concatenate(halves, axis=0))
    outs = []
    for i in range(2):
        part = total[i * half : (i + 1) * half]
        outs.append(jnp.concatenate([part, part[::-1, ::-1]], axis=0).reshape(shape))
    return outs


def neighbour_halo(cells, width, dim):
    count = lax.axis_size("seq")
    head = lax.slice_in_dim(cells, 0, width, axis=dim)
    tail = lax.slice_in_dim(cells, cells.shape[dim] - width, cells.shape[dim], axis=dim)
    from_left = lax.ppermute(tail, "seq", [(i, i + 1) for i in range(count - 1)])
    from_right = lax.ppermute(head, "seq", [(i + 1, i) for i in range(count - 1)])
    return from_left, from_right


def inside_window(rows, reach):
    panel = rows - 2 * reach
    place = lax.axis_index("seq") * panel + jnp.arange(rows, dtype=jnp.int32) - reach
    return (place >= 0) & (place < lax.axis_size("seq") * panel)


def anti_diagonal(channels):
    i = jnp.arange(channels, dtype=jnp.int32)
    return (i[:, None] + i[None, :] == channels - 1).astype(jnp.bfloat16)


def mirrored_taps(weight):
    anti = anti_diagonal(weight.shape[1])
    flipped = weight[::-1]
    left = jnp.einsum("ab,kbc->kac", anti, flipped, preferred_element_type=jnp.float32).astype(weight.dtype)
    return jnp.einsum("kab,bc->kac", left, anti, preferred_element_type=jnp.float32).astype(weight.dtype)


def both_strands(stacked, matrix, mirrored):
    channels = matrix.shape[2]
    both = product(stacked, jnp.concatenate([matrix.reshape(-1, channels), mirrored.reshape(-1, channels)], axis=1))
    return both[..., :channels] + both[..., channels:]


def taps_of(padded, dilation, rows, order):
    return jnp.concatenate(
        [lax.slice_in_dim(padded, k * dilation, k * dilation + rows, axis=1) for k in order], axis=-1
    )


def local(codes, embed, first_weight_taps, second_weight_taps, cotangent):
    one, two = FIRST_DILATION, SECOND_DILATION
    panel = codes.shape[1]
    reach_hidden = 2 * two
    reach_codes = reach_hidden + one
    code_left, code_right = neighbour_halo(codes, reach_codes, 1)
    cot_left, cot_right = neighbour_halo(cotangent, two, 1)
    codes_wide = jnp.concatenate([code_left, codes, code_right], axis=1)
    cot_wide = jnp.concatenate([cot_left, cotangent, cot_right], axis=1)

    first_mirror = mirrored_taps(first_weight_taps)
    second_mirror = mirrored_taps(second_weight_taps)

    onehot = (codes_wide[..., None] == jnp.arange(4, dtype=jnp.int32)).astype(jnp.bfloat16)
    features = product(onehot, embed).astype(jnp.bfloat16)
    rows_codes = panel + 2 * reach_codes
    features = jnp.where(inside_window(rows_codes, reach_codes)[None, :, None], features, jnp.zeros_like(features))

    rows_hidden = panel + 2 * reach_hidden
    first_stack = taps_of(features, one, rows_hidden, (0, 1, 2))
    first_activation = both_strands(first_stack, first_weight_taps, first_mirror)
    hidden = jax.nn.gelu(first_activation).astype(jnp.bfloat16)
    hidden = jnp.where(inside_window(rows_hidden, reach_hidden)[None, :, None], hidden, jnp.zeros_like(hidden))

    rows_two = panel + 2 * two
    second_stack = taps_of(hidden, two, rows_two, (0, 1, 2))
    second_activation = both_strands(second_stack, second_weight_taps, second_mirror)
    gelu_two, back_two = jax.vjp(jax.nn.gelu, second_activation)

    hidden_own = lax.slice_in_dim(hidden, reach_hidden, reach_hidden + panel, axis=1)
    block_out = (hidden_own.astype(jnp.float32) + lax.slice_in_dim(gelu_two, two, two + panel, axis=1)).astype(jnp.bfloat16)

    second_grad_wide = back_two(cot_wide.astype(jnp.float32))[0].astype(jnp.bfloat16)
    grad_stack = taps_of(second_grad_wide, two, panel, (2, 1, 0))
    flat_t = jnp.transpose(second_weight_taps, (0, 2, 1))
    mirror_t = jnp.transpose(second_mirror, (0, 2, 1))
    input_contribution = both_strands(grad_stack, flat_t, mirror_t)
    hidden_gradient = cotangent.astype(jnp.float32) + input_contribution

    first_own = lax.slice_in_dim(first_activation, reach_hidden, reach_hidden + panel, axis=1)
    _, back_one = jax.vjp(jax.nn.gelu, first_own)
    first_grad = back_one(hidden_gradient)[0].astype(jnp.bfloat16)

    second_grad_own = lax.slice_in_dim(second_grad_wide, two, two + panel, axis=1)
    second_weight_gradient = folded_term(lax.slice_in_dim(second_stack, two, two + panel, axis=1), second_grad_own)
    first_weight_gradient = folded_term(
        lax.slice_in_dim(first_stack, reach_hidden, reach_hidden + panel, axis=1), first_grad
    )
    second_weight_gradient, first_weight_gradient = unfolded_sums(second_weight_gradient, first_weight_gradient)
    return (block_out, first_weight_gradient, second_weight_gradient)


def solution(mesh):
    in_specs = (P("dp", "seq"), P(), P(), P(), P("dp", "seq", None))
    out_specs = (P("dp", "seq", None), P(), P())
    return jax.shard_map(local, mesh=mesh, in_specs=in_specs, out_specs=out_specs, check_vma=False)
```

```python
import jax
import jax.numpy as jnp
from jax import lax
from jax.sharding import PartitionSpec as P

FIRST_DILATION = 4
SECOND_DILATION = 16


def with_halo(cells, sides, width):
    for axis, dim in sides:
        count = lax.axis_size(axis)
        ends = count - 1
        head = lax.slice_in_dim(cells, 0, width, axis=dim)
        tail = lax.slice_in_dim(cells, cells.shape[dim] - width, cells.shape[dim], axis=dim)
        cells = jnp.concatenate(
            [
                lax.ppermute(tail, axis, [(i, (i + 1) % count) for i in range(ends)]),
                cells,
                lax.ppermute(head, axis, [((i + 1) % count, i) for i in range(ends)]),
            ],
            axis=dim,
        )
    return cells


def pad_rows(value, dilation):
    return with_halo(value, (("seq", 1),), dilation)


def stack_rows(padded, dilation, order):
    count_rows = padded.shape[1] - 2 * dilation
    return jnp.concatenate(
        [padded[:, k * dilation : k * dilation + count_rows] for k in order], axis=-1
    )


def product(stacked, matrix):
    shape_in = stacked.shape
    result = jnp.dot(stacked.reshape(-1, shape_in[-1]), matrix, preferred_element_type=jnp.float32)
    return result.reshape(shape_in[:-1] + (matrix.shape[1],))


def weight_term(stacked, grad):
    channels = grad.shape[-1]
    term = jnp.dot(
        stacked.reshape(-1, 3 * channels).T,
        grad.reshape(-1, channels),
        preferred_element_type=jnp.float32,
    )
    return term.reshape(3, channels, channels)


def layer_forward_pass(value, weight, dilation):
    channels = weight.shape[2]
    stacked = stack_rows(pad_rows(value, dilation), dilation, (0, 1, 2))
    flat = weight.reshape(-1, channels)
    reversed_taps = weight[::-1, ::-1, ::-1].reshape(-1, channels)
    both = product(stacked, jnp.concatenate([flat, reversed_taps], axis=1))
    return (both[..., :channels] + both[..., channels:], stacked)


def input_backward_pass(grad, weight, dilation):
    channels = weight.shape[2]
    stacked = stack_rows(pad_rows(grad, dilation), dilation, (2, 1, 0))
    flat_t = jnp.transpose(weight, (0, 2, 1)).reshape(-1, channels)
    reversed_t = jnp.transpose(weight[::-1, ::-1, ::-1], (0, 2, 1)).reshape(-1, channels)
    both = product(stacked, jnp.concatenate([flat_t, reversed_t], axis=1))
    return both[..., :channels] + both[..., channels:]


def strand_total(stacked, grad):
    term = weight_term(stacked, grad)
    return term + term[::-1, ::-1, ::-1]


def exchange_groups():
    groups = []
    for axis, shift, radix in (("dp", 0, 4), ("seq", 2, 4), ("dp", 2, 4), ("seq", 0, 4)):
        if (radix << shift) <= lax.axis_size(axis):
            groups.append((axis, shift, radix))
    return groups


def partner_pairs(axis, shift, offset):
    count = lax.axis_size(axis)
    return [(i, i ^ (offset << shift)) for i in range(count)]


def butterfly_sum(rows, scattered=2):
    kept = []
    groups = exchange_groups()
    for axis, shift, radix in groups[:scattered]:
        place = (lax.axis_index(axis) >> shift) & (radix - 1)
        width = rows.shape[0] // radix
        total = lax.dynamic_slice_in_dim(rows, place * width, width)
        for offset in range(1, radix):
            sent = lax.dynamic_slice_in_dim(rows, (place ^ offset) * width, width)
            total = total + lax.ppermute(sent, axis, partner_pairs(axis, shift, offset))
        rows = total
        kept.append((axis, shift, radix, place))
    for axis, shift, radix in groups[scattered:]:
        place = (lax.axis_index(axis) >> shift) & (radix - 1)
        pieces = [rows] + [lax.ppermute(rows, axis, partner_pairs(axis, shift, offset)) for offset in range(1, radix)]
        stacked = jnp.stack(pieces)
        total = stacked[place]
        for position in range(1, radix):
            total = total + stacked[place ^ position]
        rows = total
    for axis, shift, radix, place in reversed(kept):
        width = rows.shape[0]
        full = jnp.zeros((width * radix,) + rows.shape[1:], rows.dtype)
        full = lax.dynamic_update_slice_in_dim(full, rows, place * width, 0)
        for offset in range(1, radix):
            got = lax.ppermute(rows, axis, partner_pairs(axis, shift, offset))
            full = lax.dynamic_update_slice_in_dim(full, got, (place ^ offset) * width, 0)
        rows = full
    return rows


def folded_term(stacked, grad):
    channels = grad.shape[-1]
    term = jnp.dot(
        grad.reshape(-1, channels).T,
        stacked.reshape(-1, 3 * channels),
        preferred_element_type=jnp.float32,
    )
    half = channels // 2
    return term[:half] + term[half:][::-1, ::-1]


def unfolded_sums(first, second):
    half, width = first.shape
    lanes = width // 3
    rows = half * 3
    total = butterfly_sum(jnp.concatenate([first.reshape(rows, lanes), second.reshape(rows, lanes)], axis=0))
    outs = []
    for i in range(2):
        part = total[i * rows : (i + 1) * rows].reshape(half, width)
        full = jnp.concatenate([part, part[::-1, ::-1]], axis=0)
        outs.append(jnp.transpose(full.reshape(2 * half, 3, width // 3), (1, 2, 0)))
    return outs


def symmetric_sum(first, second):
    shape = first.shape
    flat_rows = shape[0] * shape[1]
    half = flat_rows // 2
    halves = [g.reshape(flat_rows, shape[2])[:half] for g in (first, second)]
    total = butterfly_sum(jnp.concatenate(halves, axis=0))
    outs = []
    for i in range(2):
        part = total[i * half : (i + 1) * half]
        outs.append(jnp.concatenate([part, part[::-1, ::-1]], axis=0).reshape(shape))
    return outs


def neighbour_halo(cells, width, dim):
    count = lax.axis_size("seq")
    head = lax.slice_in_dim(cells, 0, width, axis=dim)
    tail = lax.slice_in_dim(cells, cells.shape[dim] - width, cells.shape[dim], axis=dim)
    from_left = lax.ppermute(tail, "seq", [(i, i + 1) for i in range(count - 1)])
    from_right = lax.ppermute(head, "seq", [(i + 1, i) for i in range(count - 1)])
    return from_left, from_right


def inside_window(rows, reach):
    panel = rows - 2 * reach
    place = lax.axis_index("seq") * panel + jnp.arange(rows, dtype=jnp.int32) - reach
    return (place >= 0) & (place < lax.axis_size("seq") * panel)


def anti_diagonal(channels):
    i = jnp.arange(channels, dtype=jnp.int32)
    return (i[:, None] + i[None, :] == channels - 1).astype(jnp.bfloat16)


def mirrored_taps(weight):
    anti = anti_diagonal(weight.shape[1])
    flipped = weight[::-1]
    left = jnp.einsum("ab,kbc->kac", anti, flipped, preferred_element_type=jnp.float32).astype(weight.dtype)
    return jnp.einsum("kab,bc->kac", left, anti, preferred_element_type=jnp.float32).astype(weight.dtype)


def both_strands(stacked, matrix, mirrored):
    channels = matrix.shape[2]
    both = product(stacked, jnp.concatenate([matrix.reshape(-1, channels), mirrored.reshape(-1, channels)], axis=1))
    return both[..., :channels] + both[..., channels:]


def taps_of(padded, dilation, rows, order):
    return jnp.concatenate(
        [lax.slice_in_dim(padded, k * dilation, k * dilation + rows, axis=1) for k in order], axis=-1
    )


def local(codes, embed, first_weight_taps, second_weight_taps, cotangent):
    one, two = FIRST_DILATION, SECOND_DILATION
    panel = codes.shape[1]
    reach_hidden = 2 * two
    reach_codes = reach_hidden + one
    code_left, code_right = neighbour_halo(codes, reach_codes, 1)
    cot_left, cot_right = neighbour_halo(cotangent, two, 1)
    codes_wide = jnp.concatenate([code_left, codes, code_right], axis=1)
    cot_wide = jnp.concatenate([cot_left, cotangent, cot_right], axis=1)

    first_mirror = mirrored_taps(first_weight_taps)
    second_mirror = mirrored_taps(second_weight_taps)

    onehot = (codes_wide[..., None] == jnp.arange(4, dtype=jnp.int32)).astype(jnp.bfloat16)
    features = product(onehot, embed).astype(jnp.bfloat16)
    rows_codes = panel + 2 * reach_codes
    features = jnp.where(inside_window(rows_codes, reach_codes)[None, :, None], features, jnp.zeros_like(features))

    rows_hidden = panel + 2 * reach_hidden
    first_stack = taps_of(features, one, rows_hidden, (0, 1, 2))
    first_activation = both_strands(first_stack, first_weight_taps, first_mirror)
    hidden = jax.nn.gelu(first_activation).astype(jnp.bfloat16)
    hidden = jnp.where(inside_window(rows_hidden, reach_hidden)[None, :, None], hidden, jnp.zeros_like(hidden))

    rows_two = panel + 2 * two
    second_stack = taps_of(hidden, two, rows_two, (0, 1, 2))
    second_activation = both_strands(second_stack, second_weight_taps, second_mirror)
    gelu_two, back_two = jax.vjp(jax.nn.gelu, second_activation)

    hidden_own = lax.slice_in_dim(hidden, reach_hidden, reach_hidden + panel, axis=1)
    block_out = (hidden_own.astype(jnp.float32) + lax.slice_in_dim(gelu_two, two, two + panel, axis=1)).astype(jnp.bfloat16)

    second_grad_wide = back_two(cot_wide.astype(jnp.float32))[0].astype(jnp.bfloat16)
    grad_stack = taps_of(second_grad_wide, two, panel, (2, 1, 0))
    flat_t = jnp.transpose(second_weight_taps, (0, 2, 1))
    mirror_t = jnp.transpose(second_mirror, (0, 2, 1))
    input_contribution = both_strands(grad_stack, flat_t, mirror_t)
    hidden_gradient = cotangent.astype(jnp.float32) + input_contribution

    first_own = lax.slice_in_dim(first_activation, reach_hidden, reach_hidden + panel, axis=1)
    _, back_one = jax.vjp(jax.nn.gelu, first_own)
    first_grad = back_one(hidden_gradient)[0].astype(jnp.bfloat16)

    second_grad_own = lax.slice_in_dim(second_grad_wide, two, two + panel, axis=1)
    second_weight_gradient = folded_term(lax.slice_in_dim(second_stack, two, two + panel, axis=1), second_grad_own)
    first_weight_gradient = folded_term(
        lax.slice_in_dim(first_stack, reach_hidden, reach_hidden + panel, axis=1), first_grad
    )
    second_weight_gradient, first_weight_gradient = unfolded_sums(second_weight_gradient, first_weight_gradient)
    return (block_out, first_weight_gradient, second_weight_gradient)


def solution(mesh):
    in_specs = (P("dp", "seq"), P(), P(), P(), P("dp", "seq", None))
    out_specs = (P("dp", "seq", None), P(), P())
    return jax.shard_map(local, mesh=mesh, in_specs=in_specs, out_specs=out_specs, check_vma=False)
```

```python
import jax
import jax.numpy as jnp
from jax import lax
from jax.sharding import PartitionSpec as P

FIRST_DILATION = 4
SECOND_DILATION = 16


def with_halo(cells, sides, width):
    for axis, dim in sides:
        count = lax.axis_size(axis)
        ends = count - 1
        head = lax.slice_in_dim(cells, 0, width, axis=dim)
        tail = lax.slice_in_dim(cells, cells.shape[dim] - width, cells.shape[dim], axis=dim)
        cells = jnp.concatenate(
            [
                lax.ppermute(tail, axis, [(i, (i + 1) % count) for i in range(ends)]),
                cells,
                lax.ppermute(head, axis, [((i + 1) % count, i) for i in range(ends)]),
            ],
            axis=dim,
        )
    return cells


def pad_rows(value, dilation):
    return with_halo(value, (("seq", 1),), dilation)


def stack_rows(padded, dilation, order):
    count_rows = padded.shape[1] - 2 * dilation
    return jnp.concatenate(
        [padded[:, k * dilation : k * dilation + count_rows] for k in order], axis=-1
    )


def product(stacked, matrix):
    shape_in = stacked.shape
    result = jnp.dot(stacked.reshape(-1, shape_in[-1]), matrix, preferred_element_type=jnp.float32)
    return result.reshape(shape_in[:-1] + (matrix.shape[1],))


def weight_term(stacked, grad):
    channels = grad.shape[-1]
    term = jnp.dot(
        stacked.reshape(-1, 3 * channels).T,
        grad.reshape(-1, channels),
        preferred_element_type=jnp.float32,
    )
    return term.reshape(3, channels, channels)


def layer_forward_pass(value, weight, dilation):
    channels = weight.shape[2]
    stacked = stack_rows(pad_rows(value, dilation), dilation, (0, 1, 2))
    flat = weight.reshape(-1, channels)
    reversed_taps = weight[::-1, ::-1, ::-1].reshape(-1, channels)
    both = product(stacked, jnp.concatenate([flat, reversed_taps], axis=1))
    return (both[..., :channels] + both[..., channels:], stacked)


def input_backward_pass(grad, weight, dilation):
    channels = weight.shape[2]
    stacked = stack_rows(pad_rows(grad, dilation), dilation, (2, 1, 0))
    flat_t = jnp.transpose(weight, (0, 2, 1)).reshape(-1, channels)
    reversed_t = jnp.transpose(weight[::-1, ::-1, ::-1], (0, 2, 1)).reshape(-1, channels)
    both = product(stacked, jnp.concatenate([flat_t, reversed_t], axis=1))
    return both[..., :channels] + both[..., channels:]


def strand_total(stacked, grad):
    term = weight_term(stacked, grad)
    return term + term[::-1, ::-1, ::-1]


def exchange_groups():
    groups = []
    for axis, shift, radix in (("dp", 0, 4), ("seq", 2, 4), ("dp", 2, 4), ("seq", 0, 4)):
        if (radix << shift) <= lax.axis_size(axis):
            groups.append((axis, shift, radix))
    return groups


def partner_pairs(axis, shift, offset):
    count = lax.axis_size(axis)
    return [(i, i ^ (offset << shift)) for i in range(count)]


def butterfly_sum(rows, scattered=2):
    kept = []
    groups = exchange_groups()
    for axis, shift, radix in groups[:scattered]:
        place = (lax.axis_index(axis) >> shift) & (radix - 1)
        width = rows.shape[0] // radix
        total = lax.dynamic_slice_in_dim(rows, place * width, width)
        for offset in range(1, radix):
            sent = lax.dynamic_slice_in_dim(rows, (place ^ offset) * width, width)
            total = total + lax.ppermute(sent, axis, partner_pairs(axis, shift, offset))
        rows = total
        kept.append((axis, shift, radix, place))
    for axis, shift, radix in groups[scattered:]:
        place = (lax.axis_index(axis) >> shift) & (radix - 1)
        pieces = [rows] + [lax.ppermute(rows, axis, partner_pairs(axis, shift, offset)) for offset in range(1, radix)]
        stacked = jnp.stack(pieces)
        total = stacked[place]
        for position in range(1, radix):
            total = total + stacked[place ^ position]
        rows = total
    for axis, shift, radix, place in reversed(kept):
        width = rows.shape[0]
        full = jnp.zeros((width * radix,) + rows.shape[1:], rows.dtype)
        full = lax.dynamic_update_slice_in_dim(full, rows, place * width, 0)
        for offset in range(1, radix):
            got = lax.ppermute(rows, axis, partner_pairs(axis, shift, offset))
            full = lax.dynamic_update_slice_in_dim(full, got, (place ^ offset) * width, 0)
        rows = full
    return rows


def reversed_channels(value, keep=None):
    anti = anti_diagonal(value.shape[-1])
    if keep is not None:
        anti = anti[:, :keep]
    return jnp.einsum("btc,cd->btd", value, anti, preferred_element_type=jnp.float32).astype(value.dtype)


def folded_half(value, grad, dilation, offset):
    channels = grad.shape[-1]
    half = channels // 2
    panel = grad.shape[1]
    mirror = reversed_channels(value)
    grad_left = grad[0, :, :half]
    grad_mirror = reversed_channels(grad, half)[0]
    blocks = []
    for k in range(3):
        own = lax.slice_in_dim(value, offset + k * dilation, offset + k * dilation + panel, axis=1)[0]
        other = lax.slice_in_dim(mirror, offset + (2 - k) * dilation, offset + (2 - k) * dilation + panel, axis=1)[0]
        blocks.append(
            jnp.dot(grad_left.T, own, preferred_element_type=jnp.float32)
            + jnp.dot(grad_mirror.T, other, preferred_element_type=jnp.float32)
        )
    return jnp.concatenate(blocks, axis=0)


def unfolded_halves(first, second):
    rows, channels = first.shape
    half = rows // 3
    total = butterfly_sum(jnp.concatenate([first, second], axis=0))
    outs = []
    for i in range(2):
        part = total[i * rows : (i + 1) * rows]
        taps = [part[k * half : (k + 1) * half].T for k in range(3)]
        outs.append(jnp.stack([jnp.concatenate([taps[k], taps[2 - k][::-1, ::-1]], axis=1) for k in range(3)]))
    return outs


def folded_term(stacked, grad):
    channels = grad.shape[-1]
    term = jnp.dot(
        grad.reshape(-1, channels).T,
        stacked.reshape(-1, 3 * channels),
        preferred_element_type=jnp.float32,
    )
    half = channels // 2
    return term[:half] + term[half:][::-1, ::-1]


def unfolded_sums(first, second):
    half, width = first.shape
    lanes = width // 3
    rows = half * 3
    total = butterfly_sum(jnp.concatenate([first.reshape(rows, lanes), second.reshape(rows, lanes)], axis=0))
    outs = []
    for i in range(2):
        part = total[i * rows : (i + 1) * rows].reshape(half, width)
        full = jnp.concatenate([part, part[::-1, ::-1]], axis=0)
        outs.append(jnp.transpose(full.reshape(2 * half, 3, width // 3), (1, 2, 0)))
    return outs


def symmetric_sum(first, second):
    shape = first.shape
    flat_rows = shape[0] * shape[1]
    half = flat_rows // 2
    halves = [g.reshape(flat_rows, shape[2])[:half] for g in (first, second)]
    total = butterfly_sum(jnp.concatenate(halves, axis=0))
    outs = []
    for i in range(2):
        part = total[i * half : (i + 1) * half]
        outs.append(jnp.concatenate([part, part[::-1, ::-1]], axis=0).reshape(shape))
    return outs


def neighbour_halo(cells, width, dim):
    count = lax.axis_size("seq")
    head = lax.slice_in_dim(cells, 0, width, axis=dim)
    tail = lax.slice_in_dim(cells, cells.shape[dim] - width, cells.shape[dim], axis=dim)
    from_left = lax.ppermute(tail, "seq", [(i, i + 1) for i in range(count - 1)])
    from_right = lax.ppermute(head, "seq", [(i + 1, i) for i in range(count - 1)])
    return from_left, from_right


def inside_window(rows, reach):
    panel = rows - 2 * reach
    place = lax.axis_index("seq") * panel + jnp.arange(rows, dtype=jnp.int32) - reach
    return (place >= 0) & (place < lax.axis_size("seq") * panel)


def anti_diagonal(channels):
    i = jnp.arange(channels, dtype=jnp.int32)
    return (i[:, None] + i[None, :] == channels - 1).astype(jnp.bfloat16)


def mirrored_taps(weight):
    anti = anti_diagonal(weight.shape[1])
    flipped = weight[::-1]
    left = jnp.einsum("ab,kbc->kac", anti, flipped, preferred_element_type=jnp.float32).astype(weight.dtype)
    return jnp.einsum("kab,bc->kac", left, anti, preferred_element_type=jnp.float32).astype(weight.dtype)


def both_strands(stacked, matrix, mirrored):
    channels = matrix.shape[2]
    both = product(stacked, jnp.concatenate([matrix.reshape(-1, channels), mirrored.reshape(-1, channels)], axis=1))
    return both[..., :channels] + both[..., channels:]


def taps_of(padded, dilation, rows, order):
    return jnp.concatenate(
        [lax.slice_in_dim(padded, k * dilation, k * dilation + rows, axis=1) for k in order], axis=-1
    )


def local(codes, embed, first_weight_taps, second_weight_taps, cotangent):
    one, two = FIRST_DILATION, SECOND_DILATION
    panel = codes.shape[1]
    reach_hidden = 2 * two
    reach_codes = reach_hidden + one
    code_left, code_right = neighbour_halo(codes, reach_codes, 1)
    cot_left, cot_right = neighbour_halo(cotangent, two, 1)
    codes_wide = jnp.concatenate([code_left, codes, code_right], axis=1)
    cot_wide = jnp.concatenate([cot_left, cotangent, cot_right], axis=1)

    first_mirror = mirrored_taps(first_weight_taps)
    second_mirror = mirrored_taps(second_weight_taps)

    onehot = (codes_wide[..., None] == jnp.arange(4, dtype=jnp.int32)).astype(jnp.bfloat16)
    features = product(onehot, embed).astype(jnp.bfloat16)
    rows_codes = panel + 2 * reach_codes
    features = jnp.where(inside_window(rows_codes, reach_codes)[None, :, None], features, jnp.zeros_like(features))

    rows_hidden = panel + 2 * reach_hidden
    first_stack = taps_of(features, one, rows_hidden, (0, 1, 2))
    first_activation = both_strands(first_stack, first_weight_taps, first_mirror)
    hidden = jax.nn.gelu(first_activation).astype(jnp.bfloat16)
    hidden = jnp.where(inside_window(rows_hidden, reach_hidden)[None, :, None], hidden, jnp.zeros_like(hidden))

    rows_two = panel + 2 * two
    second_stack = taps_of(hidden, two, rows_two, (0, 1, 2))
    second_activation = both_strands(second_stack, second_weight_taps, second_mirror)
    gelu_two, back_two = jax.vjp(jax.nn.gelu, second_activation)

    hidden_own = lax.slice_in_dim(hidden, reach_hidden, reach_hidden + panel, axis=1)
    block_out = (hidden_own.astype(jnp.float32) + lax.slice_in_dim(gelu_two, two, two + panel, axis=1)).astype(jnp.bfloat16)

    second_grad_wide = back_two(cot_wide.astype(jnp.float32))[0].astype(jnp.bfloat16)
    grad_stack = taps_of(second_grad_wide, two, panel, (2, 1, 0))
    flat_t = jnp.transpose(second_weight_taps, (0, 2, 1))
    mirror_t = jnp.transpose(second_mirror, (0, 2, 1))
    input_contribution = both_strands(grad_stack, flat_t, mirror_t)
    hidden_gradient = cotangent.astype(jnp.float32) + input_contribution

    first_own = lax.slice_in_dim(first_activation, reach_hidden, reach_hidden + panel, axis=1)
    _, back_one = jax.vjp(jax.nn.gelu, first_own)
    first_grad = back_one(hidden_gradient)[0].astype(jnp.bfloat16)

    second_grad_own = lax.slice_in_dim(second_grad_wide, two, two + panel, axis=1)
    second_weight_gradient = folded_half(hidden, second_grad_own, two, reach_hidden - two)
    first_weight_gradient = folded_half(features, first_grad, one, reach_codes - one)
    second_weight_gradient, first_weight_gradient = unfolded_halves(second_weight_gradient, first_weight_gradient)
    return (block_out, first_weight_gradient, second_weight_gradient)


def solution(mesh):
    in_specs = (P("dp", "seq"), P(), P(), P(), P("dp", "seq", None))
    out_specs = (P("dp", "seq", None), P(), P())
    return jax.shard_map(local, mesh=mesh, in_specs=in_specs, out_specs=out_specs, check_vma=False)
```

```python
import jax
import jax.numpy as jnp
from jax import lax
from jax.sharding import PartitionSpec as P

FIRST_DILATION = 4
SECOND_DILATION = 16


def with_halo(cells, sides, width):
    for axis, dim in sides:
        count = lax.axis_size(axis)
        ends = count - 1
        head = lax.slice_in_dim(cells, 0, width, axis=dim)
        tail = lax.slice_in_dim(cells, cells.shape[dim] - width, cells.shape[dim], axis=dim)
        cells = jnp.concatenate(
            [
                lax.ppermute(tail, axis, [(i, (i + 1) % count) for i in range(ends)]),
                cells,
                lax.ppermute(head, axis, [((i + 1) % count, i) for i in range(ends)]),
            ],
            axis=dim,
        )
    return cells


def pad_rows(value, dilation):
    return with_halo(value, (("seq", 1),), dilation)


def stack_rows(padded, dilation, order):
    count_rows = padded.shape[1] - 2 * dilation
    return jnp.concatenate(
        [padded[:, k * dilation : k * dilation + count_rows] for k in order], axis=-1
    )


def product(stacked, matrix):
    shape_in = stacked.shape
    result = jnp.dot(stacked.reshape(-1, shape_in[-1]), matrix, preferred_element_type=jnp.float32)
    return result.reshape(shape_in[:-1] + (matrix.shape[1],))


def weight_term(stacked, grad):
    channels = grad.shape[-1]
    term = jnp.dot(
        stacked.reshape(-1, 3 * channels).T,
        grad.reshape(-1, channels),
        preferred_element_type=jnp.float32,
    )
    return term.reshape(3, channels, channels)


def layer_forward_pass(value, weight, dilation):
    channels = weight.shape[2]
    stacked = stack_rows(pad_rows(value, dilation), dilation, (0, 1, 2))
    flat = weight.reshape(-1, channels)
    reversed_taps = weight[::-1, ::-1, ::-1].reshape(-1, channels)
    both = product(stacked, jnp.concatenate([flat, reversed_taps], axis=1))
    return (both[..., :channels] + both[..., channels:], stacked)


def input_backward_pass(grad, weight, dilation):
    channels = weight.shape[2]
    stacked = stack_rows(pad_rows(grad, dilation), dilation, (2, 1, 0))
    flat_t = jnp.transpose(weight, (0, 2, 1)).reshape(-1, channels)
    reversed_t = jnp.transpose(weight[::-1, ::-1, ::-1], (0, 2, 1)).reshape(-1, channels)
    both = product(stacked, jnp.concatenate([flat_t, reversed_t], axis=1))
    return both[..., :channels] + both[..., channels:]


def strand_total(stacked, grad):
    term = weight_term(stacked, grad)
    return term + term[::-1, ::-1, ::-1]


def exchange_groups():
    groups = []
    for axis, shift, radix in (("dp", 0, 4), ("seq", 2, 4), ("dp", 2, 4), ("seq", 0, 4)):
        if (radix << shift) <= lax.axis_size(axis):
            groups.append((axis, shift, radix))
    return groups


def partner_pairs(axis, shift, offset):
    count = lax.axis_size(axis)
    return [(i, i ^ (offset << shift)) for i in range(count)]


def butterfly_sum(rows, scattered=2):
    kept = []
    groups = exchange_groups()
    for axis, shift, radix in groups[:scattered]:
        place = (lax.axis_index(axis) >> shift) & (radix - 1)
        width = rows.shape[0] // radix
        total = lax.dynamic_slice_in_dim(rows, place * width, width)
        for offset in range(1, radix):
            sent = lax.dynamic_slice_in_dim(rows, (place ^ offset) * width, width)
            total = total + lax.ppermute(sent, axis, partner_pairs(axis, shift, offset))
        rows = total
        kept.append((axis, shift, radix, place))
    for axis, shift, radix in groups[scattered:]:
        place = (lax.axis_index(axis) >> shift) & (radix - 1)
        pieces = [rows] + [lax.ppermute(rows, axis, partner_pairs(axis, shift, offset)) for offset in range(1, radix)]
        stacked = jnp.stack(pieces)
        total = stacked[place]
        for position in range(1, radix):
            total = total + stacked[place ^ position]
        rows = total
    for axis, shift, radix, place in reversed(kept):
        width = rows.shape[0]
        full = jnp.zeros((width * radix,) + rows.shape[1:], rows.dtype)
        full = lax.dynamic_update_slice_in_dim(full, rows, place * width, 0)
        for offset in range(1, radix):
            got = lax.ppermute(rows, axis, partner_pairs(axis, shift, offset))
            full = lax.dynamic_update_slice_in_dim(full, got, (place ^ offset) * width, 0)
        rows = full
    return rows


def reversed_channels(value, keep=None):
    anti = anti_diagonal(value.shape[-1])
    if keep is not None:
        anti = anti[:, :keep]
    return jnp.einsum("btc,cd->btd", value, anti, preferred_element_type=jnp.float32).astype(value.dtype)


def folded_half(value, grad, dilation, offset):
    channels = grad.shape[-1]
    half = channels // 2
    panel = grad.shape[1]
    mirror = reversed_channels(value)
    grad_left = grad[0, :, :half]
    grad_mirror = reversed_channels(grad, half)[0]
    blocks = []
    for k in range(3):
        own = lax.slice_in_dim(value, offset + k * dilation, offset + k * dilation + panel, axis=1)[0]
        other = lax.slice_in_dim(mirror, offset + (2 - k) * dilation, offset + (2 - k) * dilation + panel, axis=1)[0]
        blocks.append(
            jnp.dot(grad_left.T, own, preferred_element_type=jnp.float32)
            + jnp.dot(grad_mirror.T, other, preferred_element_type=jnp.float32)
        )
    return jnp.concatenate(blocks, axis=0)


def unfolded_halves(first, second):
    rows, channels = first.shape
    half = rows // 3
    total = butterfly_sum(jnp.concatenate([first, second], axis=0))
    outs = []
    for i in range(2):
        part = total[i * rows : (i + 1) * rows]
        taps = [part[k * half : (k + 1) * half].T for k in range(3)]
        outs.append(jnp.stack([jnp.concatenate([taps[k], taps[2 - k][::-1, ::-1]], axis=1) for k in range(3)]))
    return outs


def folded_term(stacked, grad):
    channels = grad.shape[-1]
    term = jnp.dot(
        grad.reshape(-1, channels).T,
        stacked.reshape(-1, 3 * channels),
        preferred_element_type=jnp.float32,
    )
    half = channels // 2
    return term[:half] + term[half:][::-1, ::-1]


def unfolded_sums(first, second):
    half, width = first.shape
    lanes = width // 3
    rows = half * 3
    total = butterfly_sum(jnp.concatenate([first.reshape(rows, lanes), second.reshape(rows, lanes)], axis=0))
    outs = []
    for i in range(2):
        part = total[i * rows : (i + 1) * rows].reshape(half, width)
        full = jnp.concatenate([part, part[::-1, ::-1]], axis=0)
        outs.append(jnp.transpose(full.reshape(2 * half, 3, width // 3), (1, 2, 0)))
    return outs


def symmetric_sum(first, second):
    shape = first.shape
    flat_rows = shape[0] * shape[1]
    half = flat_rows // 2
    halves = [g.reshape(flat_rows, shape[2])[:half] for g in (first, second)]
    total = butterfly_sum(jnp.concatenate(halves, axis=0))
    outs = []
    for i in range(2):
        part = total[i * half : (i + 1) * half]
        outs.append(jnp.concatenate([part, part[::-1, ::-1]], axis=0).reshape(shape))
    return outs


def neighbour_halo(cells, width, dim):
    count = lax.axis_size("seq")
    head = lax.slice_in_dim(cells, 0, width, axis=dim)
    tail = lax.slice_in_dim(cells, cells.shape[dim] - width, cells.shape[dim], axis=dim)
    from_left = lax.ppermute(tail, "seq", [(i, i + 1) for i in range(count - 1)])
    from_right = lax.ppermute(head, "seq", [(i + 1, i) for i in range(count - 1)])
    return from_left, from_right


def inside_window(rows, reach):
    panel = rows - 2 * reach
    place = lax.axis_index("seq") * panel + jnp.arange(rows, dtype=jnp.int32) - reach
    return (place >= 0) & (place < lax.axis_size("seq") * panel)


def anti_diagonal(channels):
    i = jnp.arange(channels, dtype=jnp.int32)
    return (i[:, None] + i[None, :] == channels - 1).astype(jnp.bfloat16)


def mirrored_taps(weight):
    anti = anti_diagonal(weight.shape[1])
    flipped = weight[::-1]
    left = jnp.einsum("ab,kbc->kac", anti, flipped, preferred_element_type=jnp.float32).astype(weight.dtype)
    return jnp.einsum("kab,bc->kac", left, anti, preferred_element_type=jnp.float32).astype(weight.dtype)


def both_strands(stacked, matrix, mirrored):
    channels = matrix.shape[2]
    both = product(stacked, jnp.concatenate([matrix.reshape(-1, channels), mirrored.reshape(-1, channels)], axis=1))
    return both[..., :channels] + both[..., channels:]


def taps_of(padded, dilation, rows, order):
    return jnp.concatenate(
        [lax.slice_in_dim(padded, k * dilation, k * dilation + rows, axis=1) for k in order], axis=-1
    )


def local(codes, embed, first_weight_taps, second_weight_taps, cotangent):
    one, two = FIRST_DILATION, SECOND_DILATION
    panel = codes.shape[1]
    reach_hidden = 2 * two
    reach_codes = reach_hidden + one
    channels = cotangent.shape[2]
    codes_row = codes.astype(cotangent.dtype)
    head = jnp.concatenate(
        [cotangent[:, :two], jnp.pad(codes_row[:, :reach_codes], ((0, 0), (0, channels - reach_codes)))[:, None]], axis=1
    )
    tail = jnp.concatenate(
        [cotangent[:, panel - two :], jnp.pad(codes_row[:, panel - reach_codes :], ((0, 0), (0, channels - reach_codes)))[:, None]],
        axis=1,
    )
    count = lax.axis_size("seq")
    from_left = lax.ppermute(tail, "seq", [(i, i + 1) for i in range(count - 1)])
    from_right = lax.ppermute(head, "seq", [(i + 1, i) for i in range(count - 1)])
    cot_left, cot_right = from_left[:, :two], from_right[:, :two]
    code_left = from_left[:, two, :reach_codes].astype(jnp.int32)
    code_right = from_right[:, two, :reach_codes].astype(jnp.int32)
    codes_wide = jnp.concatenate([code_left, codes, code_right], axis=1)
    cot_wide = jnp.concatenate([cot_left, cotangent, cot_right], axis=1)

    first_mirror = mirrored_taps(first_weight_taps)
    second_mirror = mirrored_taps(second_weight_taps)

    onehot = (codes_wide[..., None] == jnp.arange(4, dtype=jnp.int32)).astype(jnp.bfloat16)
    features = product(onehot, embed).astype(jnp.bfloat16)
    rows_codes = panel + 2 * reach_codes
    features = jnp.where(inside_window(rows_codes, reach_codes)[None, :, None], features, jnp.zeros_like(features))

    rows_hidden = panel + 2 * reach_hidden
    first_stack = taps_of(features, one, rows_hidden, (0, 1, 2))
    first_activation = both_strands(first_stack, first_weight_taps, first_mirror)
    hidden = jax.nn.gelu(first_activation).astype(jnp.bfloat16)
    hidden = jnp.where(inside_window(rows_hidden, reach_hidden)[None, :, None], hidden, jnp.zeros_like(hidden))

    rows_two = panel + 2 * two
    second_stack = taps_of(hidden, two, rows_two, (0, 1, 2))
    second_activation = both_strands(second_stack, second_weight_taps, second_mirror)
    gelu_two, back_two = jax.vjp(jax.nn.gelu, second_activation)

    hidden_own = lax.slice_in_dim(hidden, reach_hidden, reach_hidden + panel, axis=1)
    block_out = (hidden_own.astype(jnp.float32) + lax.slice_in_dim(gelu_two, two, two + panel, axis=1)).astype(jnp.bfloat16)

    second_grad_wide = back_two(cot_wide.astype(jnp.float32))[0].astype(jnp.bfloat16)
    grad_stack = taps_of(second_grad_wide, two, panel, (2, 1, 0))
    flat_t = jnp.transpose(second_weight_taps, (0, 2, 1))
    mirror_t = jnp.transpose(second_mirror, (0, 2, 1))
    input_contribution = both_strands(grad_stack, flat_t, mirror_t)
    hidden_gradient = cotangent.astype(jnp.float32) + input_contribution

    first_own = lax.slice_in_dim(first_activation, reach_hidden, reach_hidden + panel, axis=1)
    _, back_one = jax.vjp(jax.nn.gelu, first_own)
    first_grad = back_one(hidden_gradient)[0].astype(jnp.bfloat16)

    second_grad_own = lax.slice_in_dim(second_grad_wide, two, two + panel, axis=1)
    second_weight_gradient = folded_half(hidden, second_grad_own, two, reach_hidden - two)
    first_weight_gradient = folded_half(features, first_grad, one, reach_codes - one)
    second_weight_gradient, first_weight_gradient = unfolded_halves(second_weight_gradient, first_weight_gradient)
    return (block_out, first_weight_gradient, second_weight_gradient)


def solution(mesh):
    in_specs = (P("dp", "seq"), P(), P(), P(), P("dp", "seq", None))
    out_specs = (P("dp", "seq", None), P(), P())
    return jax.shard_map(local, mesh=mesh, in_specs=in_specs, out_specs=out_specs, check_vma=False)
```

```python
import jax
import jax.numpy as jnp
from jax import lax
from jax.sharding import PartitionSpec as P

FIRST_DILATION = 4
SECOND_DILATION = 16


def with_halo(cells, sides, width):
    for axis, dim in sides:
        count = lax.axis_size(axis)
        ends = count - 1
        head = lax.slice_in_dim(cells, 0, width, axis=dim)
        tail = lax.slice_in_dim(cells, cells.shape[dim] - width, cells.shape[dim], axis=dim)
        cells = jnp.concatenate(
            [
                lax.ppermute(tail, axis, [(i, (i + 1) % count) for i in range(ends)]),
                cells,
                lax.ppermute(head, axis, [((i + 1) % count, i) for i in range(ends)]),
            ],
            axis=dim,
        )
    return cells


def pad_rows(value, dilation):
    return with_halo(value, (("seq", 1),), dilation)


def stack_rows(padded, dilation, order):
    count_rows = padded.shape[1] - 2 * dilation
    return jnp.concatenate(
        [padded[:, k * dilation : k * dilation + count_rows] for k in order], axis=-1
    )


def product(stacked, matrix):
    shape_in = stacked.shape
    result = jnp.dot(stacked.reshape(-1, shape_in[-1]), matrix, preferred_element_type=jnp.float32)
    return result.reshape(shape_in[:-1] + (matrix.shape[1],))


def weight_term(stacked, grad):
    channels = grad.shape[-1]
    term = jnp.dot(
        stacked.reshape(-1, 3 * channels).T,
        grad.reshape(-1, channels),
        preferred_element_type=jnp.float32,
    )
    return term.reshape(3, channels, channels)


def layer_forward_pass(value, weight, dilation):
    channels = weight.shape[2]
    stacked = stack_rows(pad_rows(value, dilation), dilation, (0, 1, 2))
    flat = weight.reshape(-1, channels)
    reversed_taps = weight[::-1, ::-1, ::-1].reshape(-1, channels)
    both = product(stacked, jnp.concatenate([flat, reversed_taps], axis=1))
    return (both[..., :channels] + both[..., channels:], stacked)


def input_backward_pass(grad, weight, dilation):
    channels = weight.shape[2]
    stacked = stack_rows(pad_rows(grad, dilation), dilation, (2, 1, 0))
    flat_t = jnp.transpose(weight, (0, 2, 1)).reshape(-1, channels)
    reversed_t = jnp.transpose(weight[::-1, ::-1, ::-1], (0, 2, 1)).reshape(-1, channels)
    both = product(stacked, jnp.concatenate([flat_t, reversed_t], axis=1))
    return both[..., :channels] + both[..., channels:]


def strand_total(stacked, grad):
    term = weight_term(stacked, grad)
    return term + term[::-1, ::-1, ::-1]


def exchange_groups():
    groups = []
    for axis, shift, radix in (("dp", 0, 4), ("seq", 2, 4), ("dp", 2, 4), ("seq", 0, 4)):
        if (radix << shift) <= lax.axis_size(axis):
            groups.append((axis, shift, radix))
    return groups


def partner_pairs(axis, shift, offset):
    count = lax.axis_size(axis)
    return [(i, i ^ (offset << shift)) for i in range(count)]


def butterfly_sum(rows, scattered=2):
    kept = []
    groups = exchange_groups()
    for axis, shift, radix in groups[:scattered]:
        place = (lax.axis_index(axis) >> shift) & (radix - 1)
        width = rows.shape[0] // radix
        total = lax.dynamic_slice_in_dim(rows, place * width, width)
        for offset in range(1, radix):
            sent = lax.dynamic_slice_in_dim(rows, (place ^ offset) * width, width)
            total = total + lax.ppermute(sent, axis, partner_pairs(axis, shift, offset))
        rows = total
        kept.append((axis, shift, radix, place))
    for axis, shift, radix in groups[scattered:]:
        place = (lax.axis_index(axis) >> shift) & (radix - 1)
        pieces = [rows] + [lax.ppermute(rows, axis, partner_pairs(axis, shift, offset)) for offset in range(1, radix)]
        stacked = jnp.stack(pieces)
        total = stacked[place]
        for position in range(1, radix):
            total = total + stacked[place ^ position]
        rows = total
    for axis, shift, radix, place in reversed(kept):
        width = rows.shape[0]
        pieces = [rows] + [lax.ppermute(rows, axis, partner_pairs(axis, shift, offset)) for offset in range(1, radix)]
        order = jnp.arange(radix, dtype=jnp.int32) ^ place
        rows = jnp.take(jnp.stack(pieces), order, axis=0).reshape((width * radix,) + rows.shape[1:])
    return rows


def reversed_channels(value, keep=None):
    anti = anti_diagonal(value.shape[-1])
    if keep is not None:
        anti = anti[:, :keep]
    return jnp.einsum("btc,cd->btd", value, anti, preferred_element_type=jnp.float32).astype(value.dtype)


def folded_half(value, grad, dilation, offset):
    channels = grad.shape[-1]
    half = channels // 2
    panel = grad.shape[1]
    mirror = reversed_channels(value)
    grad_left = grad[0, :, :half]
    grad_mirror = reversed_channels(grad, half)[0]
    blocks = []
    for k in range(3):
        own = lax.slice_in_dim(value, offset + k * dilation, offset + k * dilation + panel, axis=1)[0]
        other = lax.slice_in_dim(mirror, offset + (2 - k) * dilation, offset + (2 - k) * dilation + panel, axis=1)[0]
        blocks.append(
            jnp.dot(grad_left.T, own, preferred_element_type=jnp.float32)
            + jnp.dot(grad_mirror.T, other, preferred_element_type=jnp.float32)
        )
    return jnp.concatenate(blocks, axis=0)


def unfolded_halves(first, second):
    rows, channels = first.shape
    half = rows // 3
    total = butterfly_sum(jnp.concatenate([first, second], axis=0))
    outs = []
    for i in range(2):
        part = total[i * rows : (i + 1) * rows]
        taps = [part[k * half : (k + 1) * half].T for k in range(3)]
        outs.append(jnp.stack([jnp.concatenate([taps[k], taps[2 - k][::-1, ::-1]], axis=1) for k in range(3)]))
    return outs


def folded_term(stacked, grad):
    channels = grad.shape[-1]
    term = jnp.dot(
        grad.reshape(-1, channels).T,
        stacked.reshape(-1, 3 * channels),
        preferred_element_type=jnp.float32,
    )
    half = channels // 2
    return term[:half] + term[half:][::-1, ::-1]


def unfolded_sums(first, second):
    half, width = first.shape
    lanes = width // 3
    rows = half * 3
    total = butterfly_sum(jnp.concatenate([first.reshape(rows, lanes), second.reshape(rows, lanes)], axis=0))
    outs = []
    for i in range(2):
        part = total[i * rows : (i + 1) * rows].reshape(half, width)
        full = jnp.concatenate([part, part[::-1, ::-1]], axis=0)
        outs.append(jnp.transpose(full.reshape(2 * half, 3, width // 3), (1, 2, 0)))
    return outs


def symmetric_sum(first, second):
    shape = first.shape
    flat_rows = shape[0] * shape[1]
    half = flat_rows // 2
    halves = [g.reshape(flat_rows, shape[2])[:half] for g in (first, second)]
    total = butterfly_sum(jnp.concatenate(halves, axis=0))
    outs = []
    for i in range(2):
        part = total[i * half : (i + 1) * half]
        outs.append(jnp.concatenate([part, part[::-1, ::-1]], axis=0).reshape(shape))
    return outs


def neighbour_halo(cells, width, dim):
    count = lax.axis_size("seq")
    head = lax.slice_in_dim(cells, 0, width, axis=dim)
    tail = lax.slice_in_dim(cells, cells.shape[dim] - width, cells.shape[dim], axis=dim)
    from_left = lax.ppermute(tail, "seq", [(i, i + 1) for i in range(count - 1)])
    from_right = lax.ppermute(head, "seq", [(i + 1, i) for i in range(count - 1)])
    return from_left, from_right


def inside_window(rows, reach):
    panel = rows - 2 * reach
    place = lax.axis_index("seq") * panel + jnp.arange(rows, dtype=jnp.int32) - reach
    return (place >= 0) & (place < lax.axis_size("seq") * panel)


def anti_diagonal(channels):
    i = jnp.arange(channels, dtype=jnp.int32)
    return (i[:, None] + i[None, :] == channels - 1).astype(jnp.bfloat16)


def mirrored_taps(weight):
    anti = anti_diagonal(weight.shape[1])
    flipped = weight[::-1]
    left = jnp.einsum("ab,kbc->kac", anti, flipped, preferred_element_type=jnp.float32).astype(weight.dtype)
    return jnp.einsum("kab,bc->kac", left, anti, preferred_element_type=jnp.float32).astype(weight.dtype)


def both_strands(stacked, matrix, mirrored):
    channels = matrix.shape[2]
    both = product(stacked, jnp.concatenate([matrix.reshape(-1, channels), mirrored.reshape(-1, channels)], axis=1))
    return both[..., :channels] + both[..., channels:]


def taps_of(padded, dilation, rows, order):
    return jnp.concatenate(
        [lax.slice_in_dim(padded, k * dilation, k * dilation + rows, axis=1) for k in order], axis=-1
    )


def local(codes, embed, first_weight_taps, second_weight_taps, cotangent):
    one, two = FIRST_DILATION, SECOND_DILATION
    panel = codes.shape[1]
    reach_hidden = 2 * two
    reach_codes = reach_hidden + one
    channels = cotangent.shape[2]
    codes_row = codes.astype(cotangent.dtype)
    head = jnp.concatenate(
        [cotangent[:, :two], jnp.pad(codes_row[:, :reach_codes], ((0, 0), (0, channels - reach_codes)))[:, None]], axis=1
    )
    tail = jnp.concatenate(
        [cotangent[:, panel - two :], jnp.pad(codes_row[:, panel - reach_codes :], ((0, 0), (0, channels - reach_codes)))[:, None]],
        axis=1,
    )
    count = lax.axis_size("seq")
    from_left = lax.ppermute(tail, "seq", [(i, i + 1) for i in range(count - 1)])
    from_right = lax.ppermute(head, "seq", [(i + 1, i) for i in range(count - 1)])
    cot_left, cot_right = from_left[:, :two], from_right[:, :two]
    code_left = from_left[:, two, :reach_codes].astype(jnp.int32)
    code_right = from_right[:, two, :reach_codes].astype(jnp.int32)
    codes_wide = jnp.concatenate([code_left, codes, code_right], axis=1)
    cot_wide = jnp.concatenate([cot_left, cotangent, cot_right], axis=1)

    first_mirror = mirrored_taps(first_weight_taps)
    second_mirror = mirrored_taps(second_weight_taps)

    onehot = (codes_wide[..., None] == jnp.arange(4, dtype=jnp.int32)).astype(jnp.bfloat16)
    features = product(onehot, embed).astype(jnp.bfloat16)
    rows_codes = panel + 2 * reach_codes
    features = jnp.where(inside_window(rows_codes, reach_codes)[None, :, None], features, jnp.zeros_like(features))

    rows_hidden = panel + 2 * reach_hidden
    first_stack = taps_of(features, one, rows_hidden, (0, 1, 2))
    first_activation = both_strands(first_stack, first_weight_taps, first_mirror)
    hidden = jax.nn.gelu(first_activation).astype(jnp.bfloat16)
    hidden = jnp.where(inside_window(rows_hidden, reach_hidden)[None, :, None], hidden, jnp.zeros_like(hidden))

    rows_two = panel + 2 * two
    second_stack = taps_of(hidden, two, rows_two, (0, 1, 2))
    second_activation = both_strands(second_stack, second_weight_taps, second_mirror)
    gelu_two, back_two = jax.vjp(jax.nn.gelu, second_activation)

    hidden_own = lax.slice_in_dim(hidden, reach_hidden, reach_hidden + panel, axis=1)
    block_out = (hidden_own.astype(jnp.float32) + lax.slice_in_dim(gelu_two, two, two + panel, axis=1)).astype(jnp.bfloat16)

    second_grad_wide = back_two(cot_wide.astype(jnp.float32))[0].astype(jnp.bfloat16)
    grad_stack = taps_of(second_grad_wide, two, panel, (2, 1, 0))
    flat_t = jnp.transpose(second_weight_taps, (0, 2, 1))
    mirror_t = jnp.transpose(second_mirror, (0, 2, 1))
    input_contribution = both_strands(grad_stack, flat_t, mirror_t)
    hidden_gradient = cotangent.astype(jnp.float32) + input_contribution

    first_own = lax.slice_in_dim(first_activation, reach_hidden, reach_hidden + panel, axis=1)
    _, back_one = jax.vjp(jax.nn.gelu, first_own)
    first_grad = back_one(hidden_gradient)[0].astype(jnp.bfloat16)

    second_grad_own = lax.slice_in_dim(second_grad_wide, two, two + panel, axis=1)
    second_weight_gradient = folded_half(hidden, second_grad_own, two, reach_hidden - two)
    first_weight_gradient = folded_half(features, first_grad, one, reach_codes - one)
    second_weight_gradient, first_weight_gradient = unfolded_halves(second_weight_gradient, first_weight_gradient)
    return (block_out, first_weight_gradient, second_weight_gradient)


def solution(mesh):
    in_specs = (P("dp", "seq"), P(), P(), P(), P("dp", "seq", None))
    out_specs = (P("dp", "seq", None), P(), P())
    return jax.shard_map(local, mesh=mesh, in_specs=in_specs, out_specs=out_specs, check_vma=False)
```

```python
import jax
import jax.numpy as jnp
from jax import lax
from jax.sharding import PartitionSpec as P

FIRST_DILATION = 4
SECOND_DILATION = 16


def with_halo(cells, sides, width):
    for axis, dim in sides:
        count = lax.axis_size(axis)
        ends = count - 1
        head = lax.slice_in_dim(cells, 0, width, axis=dim)
        tail = lax.slice_in_dim(cells, cells.shape[dim] - width, cells.shape[dim], axis=dim)
        cells = jnp.concatenate(
            [
                lax.ppermute(tail, axis, [(i, (i + 1) % count) for i in range(ends)]),
                cells,
                lax.ppermute(head, axis, [((i + 1) % count, i) for i in range(ends)]),
            ],
            axis=dim,
        )
    return cells


def pad_rows(value, dilation):
    return with_halo(value, (("seq", 1),), dilation)


def stack_rows(padded, dilation, order):
    count_rows = padded.shape[1] - 2 * dilation
    return jnp.concatenate(
        [padded[:, k * dilation : k * dilation + count_rows] for k in order], axis=-1
    )


def product(stacked, matrix):
    shape_in = stacked.shape
    result = jnp.dot(stacked.reshape(-1, shape_in[-1]), matrix, preferred_element_type=jnp.float32)
    return result.reshape(shape_in[:-1] + (matrix.shape[1],))


def weight_term(stacked, grad):
    channels = grad.shape[-1]
    term = jnp.dot(
        stacked.reshape(-1, 3 * channels).T,
        grad.reshape(-1, channels),
        preferred_element_type=jnp.float32,
    )
    return term.reshape(3, channels, channels)


def layer_forward_pass(value, weight, dilation):
    channels = weight.shape[2]
    stacked = stack_rows(pad_rows(value, dilation), dilation, (0, 1, 2))
    flat = weight.reshape(-1, channels)
    reversed_taps = weight[::-1, ::-1, ::-1].reshape(-1, channels)
    both = product(stacked, jnp.concatenate([flat, reversed_taps], axis=1))
    return (both[..., :channels] + both[..., channels:], stacked)


def input_backward_pass(grad, weight, dilation):
    channels = weight.shape[2]
    stacked = stack_rows(pad_rows(grad, dilation), dilation, (2, 1, 0))
    flat_t = jnp.transpose(weight, (0, 2, 1)).reshape(-1, channels)
    reversed_t = jnp.transpose(weight[::-1, ::-1, ::-1], (0, 2, 1)).reshape(-1, channels)
    both = product(stacked, jnp.concatenate([flat_t, reversed_t], axis=1))
    return both[..., :channels] + both[..., channels:]


def strand_total(stacked, grad):
    term = weight_term(stacked, grad)
    return term + term[::-1, ::-1, ::-1]


def exchange_groups():
    groups = []
    for axis, shift, radix in (("dp", 0, 4), ("seq", 2, 4), ("dp", 2, 4), ("seq", 0, 2), ("seq", 1, 2)):
        if (radix << shift) <= lax.axis_size(axis):
            groups.append((axis, shift, radix))
    return groups


def partner_pairs(axis, shift, offset):
    count = lax.axis_size(axis)
    return [(i, i ^ (offset << shift)) for i in range(count)]


def butterfly_sum(rows, scattered=2):
    kept = []
    groups = exchange_groups()
    for axis, shift, radix in groups[:scattered]:
        place = (lax.axis_index(axis) >> shift) & (radix - 1)
        width = rows.shape[0] // radix
        total = lax.dynamic_slice_in_dim(rows, place * width, width)
        for offset in range(1, radix):
            sent = lax.dynamic_slice_in_dim(rows, (place ^ offset) * width, width)
            total = total + lax.ppermute(sent, axis, partner_pairs(axis, shift, offset))
        rows = total
        kept.append((axis, shift, radix, place))
    for axis, shift, radix in groups[scattered:]:
        place = (lax.axis_index(axis) >> shift) & (radix - 1)
        pieces = [rows] + [lax.ppermute(rows, axis, partner_pairs(axis, shift, offset)) for offset in range(1, radix)]
        stacked = jnp.stack(pieces)
        total = stacked[place]
        for position in range(1, radix):
            total = total + stacked[place ^ position]
        rows = total
    for axis, shift, radix, place in reversed(kept):
        width = rows.shape[0]
        pieces = [rows] + [lax.ppermute(rows, axis, partner_pairs(axis, shift, offset)) for offset in range(1, radix)]
        order = jnp.arange(radix, dtype=jnp.int32) ^ place
        rows = jnp.take(jnp.stack(pieces), order, axis=0).reshape((width * radix,) + rows.shape[1:])
    return rows


def reversed_channels(value, keep=None):
    anti = anti_diagonal(value.shape[-1])
    if keep is not None:
        anti = anti[:, :keep]
    return jnp.einsum("btc,cd->btd", value, anti, preferred_element_type=jnp.float32).astype(value.dtype)


def folded_half(value, grad, dilation, offset):
    channels = grad.shape[-1]
    half = channels // 2
    panel = grad.shape[1]
    mirror = reversed_channels(value)
    grad_left = grad[0, :, :half]
    grad_mirror = reversed_channels(grad, half)[0]
    blocks = []
    for k in range(3):
        own = lax.slice_in_dim(value, offset + k * dilation, offset + k * dilation + panel, axis=1)[0]
        other = lax.slice_in_dim(mirror, offset + (2 - k) * dilation, offset + (2 - k) * dilation + panel, axis=1)[0]
        blocks.append(
            jnp.dot(grad_left.T, own, preferred_element_type=jnp.float32)
            + jnp.dot(grad_mirror.T, other, preferred_element_type=jnp.float32)
        )
    return jnp.concatenate(blocks, axis=0)


def unfolded_halves(first, second):
    rows, channels = first.shape
    half = rows // 3
    total = butterfly_sum(jnp.concatenate([first, second], axis=0))
    outs = []
    for i in range(2):
        part = total[i * rows : (i + 1) * rows]
        taps = [part[k * half : (k + 1) * half].T for k in range(3)]
        outs.append(jnp.stack([jnp.concatenate([taps[k], taps[2 - k][::-1, ::-1]], axis=1) for k in range(3)]))
    return outs


def folded_term(stacked, grad):
    channels = grad.shape[-1]
    term = jnp.dot(
        grad.reshape(-1, channels).T,
        stacked.reshape(-1, 3 * channels),
        preferred_element_type=jnp.float32,
    )
    half = channels // 2
    return term[:half] + term[half:][::-1, ::-1]


def unfolded_sums(first, second):
    half, width = first.shape
    lanes = width // 3
    rows = half * 3
    total = butterfly_sum(jnp.concatenate([first.reshape(rows, lanes), second.reshape(rows, lanes)], axis=0))
    outs = []
    for i in range(2):
        part = total[i * rows : (i + 1) * rows].reshape(half, width)
        full = jnp.concatenate([part, part[::-1, ::-1]], axis=0)
        outs.append(jnp.transpose(full.reshape(2 * half, 3, width // 3), (1, 2, 0)))
    return outs


def symmetric_sum(first, second):
    shape = first.shape
    flat_rows = shape[0] * shape[1]
    half = flat_rows // 2
    halves = [g.reshape(flat_rows, shape[2])[:half] for g in (first, second)]
    total = butterfly_sum(jnp.concatenate(halves, axis=0))
    outs = []
    for i in range(2):
        part = total[i * half : (i + 1) * half]
        outs.append(jnp.concatenate([part, part[::-1, ::-1]], axis=0).reshape(shape))
    return outs


def neighbour_halo(cells, width, dim):
    count = lax.axis_size("seq")
    head = lax.slice_in_dim(cells, 0, width, axis=dim)
    tail = lax.slice_in_dim(cells, cells.shape[dim] - width, cells.shape[dim], axis=dim)
    from_left = lax.ppermute(tail, "seq", [(i, i + 1) for i in range(count - 1)])
    from_right = lax.ppermute(head, "seq", [(i + 1, i) for i in range(count - 1)])
    return from_left, from_right


def inside_window(rows, reach):
    panel = rows - 2 * reach
    place = lax.axis_index("seq") * panel + jnp.arange(rows, dtype=jnp.int32) - reach
    return (place >= 0) & (place < lax.axis_size("seq") * panel)


def anti_diagonal(channels):
    i = jnp.arange(channels, dtype=jnp.int32)
    return (i[:, None] + i[None, :] == channels - 1).astype(jnp.bfloat16)


def mirrored_taps(weight):
    anti = anti_diagonal(weight.shape[1])
    flipped = weight[::-1]
    left = jnp.einsum("ab,kbc->kac", anti, flipped, preferred_element_type=jnp.float32).astype(weight.dtype)
    return jnp.einsum("kab,bc->kac", left, anti, preferred_element_type=jnp.float32).astype(weight.dtype)


def both_strands(stacked, matrix, mirrored):
    channels = matrix.shape[2]
    both = product(stacked, jnp.concatenate([matrix.reshape(-1, channels), mirrored.reshape(-1, channels)], axis=1))
    return both[..., :channels] + both[..., channels:]


def taps_of(padded, dilation, rows, order):
    return jnp.concatenate(
        [lax.slice_in_dim(padded, k * dilation, k * dilation + rows, axis=1) for k in order], axis=-1
    )


def local(codes, embed, first_weight_taps, second_weight_taps, cotangent):
    one, two = FIRST_DILATION, SECOND_DILATION
    panel = codes.shape[1]
    reach_hidden = 2 * two
    reach_codes = reach_hidden + one
    channels = cotangent.shape[2]
    codes_row = codes.astype(cotangent.dtype)
    head = jnp.concatenate(
        [cotangent[:, :two], jnp.pad(codes_row[:, :reach_codes], ((0, 0), (0, channels - reach_codes)))[:, None]], axis=1
    )
    tail = jnp.concatenate(
        [cotangent[:, panel - two :], jnp.pad(codes_row[:, panel - reach_codes :], ((0, 0), (0, channels - reach_codes)))[:, None]],
        axis=1,
    )
    count = lax.axis_size("seq")
    from_left = lax.ppermute(tail, "seq", [(i, i + 1) for i in range(count - 1)])
    from_right = lax.ppermute(head, "seq", [(i + 1, i) for i in range(count - 1)])
    cot_left, cot_right = from_left[:, :two], from_right[:, :two]
    code_left = from_left[:, two, :reach_codes].astype(jnp.int32)
    code_right = from_right[:, two, :reach_codes].astype(jnp.int32)
    codes_wide = jnp.concatenate([code_left, codes, code_right], axis=1)
    cot_wide = jnp.concatenate([cot_left, cotangent, cot_right], axis=1)

    first_mirror = mirrored_taps(first_weight_taps)
    second_mirror = mirrored_taps(second_weight_taps)

    onehot = (codes_wide[..., None] == jnp.arange(4, dtype=jnp.int32)).astype(jnp.bfloat16)
    features = product(onehot, embed).astype(jnp.bfloat16)
    rows_codes = panel + 2 * reach_codes
    features = jnp.where(inside_window(rows_codes, reach_codes)[None, :, None], features, jnp.zeros_like(features))

    rows_hidden = panel + 2 * reach_hidden
    first_stack = taps_of(features, one, rows_hidden, (0, 1, 2))
    first_activation = both_strands(first_stack, first_weight_taps, first_mirror)
    hidden = jax.nn.gelu(first_activation).astype(jnp.bfloat16)
    hidden = jnp.where(inside_window(rows_hidden, reach_hidden)[None, :, None], hidden, jnp.zeros_like(hidden))

    rows_two = panel + 2 * two
    second_stack = taps_of(hidden, two, rows_two, (0, 1, 2))
    second_activation = both_strands(second_stack, second_weight_taps, second_mirror)
    gelu_two, back_two = jax.vjp(jax.nn.gelu, second_activation)

    hidden_own = lax.slice_in_dim(hidden, reach_hidden, reach_hidden + panel, axis=1)
    block_out = (hidden_own.astype(jnp.float32) + lax.slice_in_dim(gelu_two, two, two + panel, axis=1)).astype(jnp.bfloat16)

    second_grad_wide = back_two(cot_wide.astype(jnp.float32))[0].astype(jnp.bfloat16)
    grad_stack = taps_of(second_grad_wide, two, panel, (2, 1, 0))
    flat_t = jnp.transpose(second_weight_taps, (0, 2, 1))
    mirror_t = jnp.transpose(second_mirror, (0, 2, 1))
    input_contribution = both_strands(grad_stack, flat_t, mirror_t)
    hidden_gradient = cotangent.astype(jnp.float32) + input_contribution

    first_own = lax.slice_in_dim(first_activation, reach_hidden, reach_hidden + panel, axis=1)
    _, back_one = jax.vjp(jax.nn.gelu, first_own)
    first_grad = back_one(hidden_gradient)[0].astype(jnp.bfloat16)

    second_grad_own = lax.slice_in_dim(second_grad_wide, two, two + panel, axis=1)
    second_weight_gradient = folded_half(hidden, second_grad_own, two, reach_hidden - two)
    first_weight_gradient = folded_half(features, first_grad, one, reach_codes - one)
    second_weight_gradient, first_weight_gradient = unfolded_halves(second_weight_gradient, first_weight_gradient)
    return (block_out, first_weight_gradient, second_weight_gradient)


def solution(mesh):
    in_specs = (P("dp", "seq"), P(), P(), P(), P("dp", "seq", None))
    out_specs = (P("dp", "seq", None), P(), P())
    return jax.shard_map(local, mesh=mesh, in_specs=in_specs, out_specs=out_specs, check_vma=False)
```

```python
import jax
import jax.numpy as jnp
from jax import lax
from jax.sharding import PartitionSpec as P

FIRST_DILATION = 4
SECOND_DILATION = 16


def with_halo(cells, sides, width):
    for axis, dim in sides:
        count = lax.axis_size(axis)
        ends = count - 1
        head = lax.slice_in_dim(cells, 0, width, axis=dim)
        tail = lax.slice_in_dim(cells, cells.shape[dim] - width, cells.shape[dim], axis=dim)
        cells = jnp.concatenate(
            [
                lax.ppermute(tail, axis, [(i, (i + 1) % count) for i in range(ends)]),
                cells,
                lax.ppermute(head, axis, [((i + 1) % count, i) for i in range(ends)]),
            ],
            axis=dim,
        )
    return cells


def pad_rows(value, dilation):
    return with_halo(value, (("seq", 1),), dilation)


def stack_rows(padded, dilation, order):
    count_rows = padded.shape[1] - 2 * dilation
    return jnp.concatenate(
        [padded[:, k * dilation : k * dilation + count_rows] for k in order], axis=-1
    )


def product(stacked, matrix):
    shape_in = stacked.shape
    result = jnp.dot(stacked.reshape(-1, shape_in[-1]), matrix, preferred_element_type=jnp.float32)
    return result.reshape(shape_in[:-1] + (matrix.shape[1],))


def weight_term(stacked, grad):
    channels = grad.shape[-1]
    term = jnp.dot(
        stacked.reshape(-1, 3 * channels).T,
        grad.reshape(-1, channels),
        preferred_element_type=jnp.float32,
    )
    return term.reshape(3, channels, channels)


def layer_forward_pass(value, weight, dilation):
    channels = weight.shape[2]
    stacked = stack_rows(pad_rows(value, dilation), dilation, (0, 1, 2))
    flat = weight.reshape(-1, channels)
    reversed_taps = weight[::-1, ::-1, ::-1].reshape(-1, channels)
    both = product(stacked, jnp.concatenate([flat, reversed_taps], axis=1))
    return (both[..., :channels] + both[..., channels:], stacked)


def input_backward_pass(grad, weight, dilation):
    channels = weight.shape[2]
    stacked = stack_rows(pad_rows(grad, dilation), dilation, (2, 1, 0))
    flat_t = jnp.transpose(weight, (0, 2, 1)).reshape(-1, channels)
    reversed_t = jnp.transpose(weight[::-1, ::-1, ::-1], (0, 2, 1)).reshape(-1, channels)
    both = product(stacked, jnp.concatenate([flat_t, reversed_t], axis=1))
    return both[..., :channels] + both[..., channels:]


def strand_total(stacked, grad):
    term = weight_term(stacked, grad)
    return term + term[::-1, ::-1, ::-1]


def exchange_groups():
    groups = []
    for axis, shift, radix in (("dp", 0, 4), ("seq", 2, 4), ("dp", 2, 4), ("seq", 0, 2), ("seq", 1, 2)):
        if (radix << shift) <= lax.axis_size(axis):
            groups.append((axis, shift, radix))
    return groups


def partner_pairs(axis, shift, offset):
    count = lax.axis_size(axis)
    return [(i, i ^ (offset << shift)) for i in range(count)]


def butterfly_sum(rows, scattered=2):
    kept = []
    groups = exchange_groups()
    for axis, shift, radix in groups[:scattered]:
        place = (lax.axis_index(axis) >> shift) & (radix - 1)
        width = rows.shape[0] // radix
        total = lax.dynamic_slice_in_dim(rows, place * width, width)
        for offset in range(1, radix):
            sent = lax.dynamic_slice_in_dim(rows, (place ^ offset) * width, width)
            total = total + lax.ppermute(sent, axis, partner_pairs(axis, shift, offset))
        rows = total
        kept.append((axis, shift, radix, place))
    for axis, shift, radix in groups[scattered:]:
        place = (lax.axis_index(axis) >> shift) & (radix - 1)
        pieces = [rows] + [lax.ppermute(rows, axis, partner_pairs(axis, shift, offset)) for offset in range(1, radix)]
        stacked = jnp.stack(pieces)
        total = stacked[place]
        for position in range(1, radix):
            total = total + stacked[place ^ position]
        rows = total
    for axis, shift, radix, place in reversed(kept):
        width = rows.shape[0]
        pieces = [rows] + [lax.ppermute(rows, axis, partner_pairs(axis, shift, offset)) for offset in range(1, radix)]
        order = jnp.arange(radix, dtype=jnp.int32) ^ place
        rows = jnp.take(jnp.stack(pieces), order, axis=0).reshape((width * radix,) + rows.shape[1:])
    return rows


def reversed_channels(value, keep=None):
    anti = anti_diagonal(value.shape[-1])
    if keep is not None:
        anti = anti[:, :keep]
    return jnp.einsum("btc,cd->btd", value, anti, preferred_element_type=jnp.float32).astype(value.dtype)


def folded_half(value, grad, dilation, offset):
    channels = grad.shape[-1]
    half = channels // 2
    panel = grad.shape[1]
    mirror = reversed_channels(value)
    grad_left = grad[0, :, :half]
    grad_mirror = reversed_channels(grad, half)[0]
    blocks = []
    for k in range(3):
        own = lax.slice_in_dim(value, offset + k * dilation, offset + k * dilation + panel, axis=1)[0]
        other = lax.slice_in_dim(mirror, offset + (2 - k) * dilation, offset + (2 - k) * dilation + panel, axis=1)[0]
        blocks.append(
            jnp.dot(grad_left.T, own, preferred_element_type=jnp.float32)
            + jnp.dot(grad_mirror.T, other, preferred_element_type=jnp.float32)
        )
    return jnp.concatenate(blocks, axis=0)


def unfolded_halves(first, second):
    rows, channels = first.shape
    half = rows // 3
    totals = [butterfly_sum(first), butterfly_sum(second)]
    outs = []
    for i in range(2):
        part = totals[i]
        taps = [part[k * half : (k + 1) * half].T for k in range(3)]
        outs.append(jnp.stack([jnp.concatenate([taps[k], taps[2 - k][::-1, ::-1]], axis=1) for k in range(3)]))
    return outs


def folded_term(stacked, grad):
    channels = grad.shape[-1]
    term = jnp.dot(
        grad.reshape(-1, channels).T,
        stacked.reshape(-1, 3 * channels),
        preferred_element_type=jnp.float32,
    )
    half = channels // 2
    return term[:half] + term[half:][::-1, ::-1]


def unfolded_sums(first, second):
    half, width = first.shape
    lanes = width // 3
    rows = half * 3
    total = butterfly_sum(jnp.concatenate([first.reshape(rows, lanes), second.reshape(rows, lanes)], axis=0))
    outs = []
    for i in range(2):
        part = total[i * rows : (i + 1) * rows].reshape(half, width)
        full = jnp.concatenate([part, part[::-1, ::-1]], axis=0)
        outs.append(jnp.transpose(full.reshape(2 * half, 3, width // 3), (1, 2, 0)))
    return outs


def symmetric_sum(first, second):
    shape = first.shape
    flat_rows = shape[0] * shape[1]
    half = flat_rows // 2
    halves = [g.reshape(flat_rows, shape[2])[:half] for g in (first, second)]
    total = butterfly_sum(jnp.concatenate(halves, axis=0))
    outs = []
    for i in range(2):
        part = total[i * half : (i + 1) * half]
        outs.append(jnp.concatenate([part, part[::-1, ::-1]], axis=0).reshape(shape))
    return outs


def neighbour_halo(cells, width, dim):
    count = lax.axis_size("seq")
    head = lax.slice_in_dim(cells, 0, width, axis=dim)
    tail = lax.slice_in_dim(cells, cells.shape[dim] - width, cells.shape[dim], axis=dim)
    from_left = lax.ppermute(tail, "seq", [(i, i + 1) for i in range(count - 1)])
    from_right = lax.ppermute(head, "seq", [(i + 1, i) for i in range(count - 1)])
    return from_left, from_right


def inside_window(rows, reach):
    panel = rows - 2 * reach
    place = lax.axis_index("seq") * panel + jnp.arange(rows, dtype=jnp.int32) - reach
    return (place >= 0) & (place < lax.axis_size("seq") * panel)


def anti_diagonal(channels):
    i = jnp.arange(channels, dtype=jnp.int32)
    return (i[:, None] + i[None, :] == channels - 1).astype(jnp.bfloat16)


def mirrored_taps(weight):
    anti = anti_diagonal(weight.shape[1])
    flipped = weight[::-1]
    left = jnp.einsum("ab,kbc->kac", anti, flipped, preferred_element_type=jnp.float32).astype(weight.dtype)
    return jnp.einsum("kab,bc->kac", left, anti, preferred_element_type=jnp.float32).astype(weight.dtype)


def both_strands(stacked, matrix, mirrored):
    channels = matrix.shape[2]
    both = product(stacked, jnp.concatenate([matrix.reshape(-1, channels), mirrored.reshape(-1, channels)], axis=1))
    return both[..., :channels] + both[..., channels:]


def taps_of(padded, dilation, rows, order):
    return jnp.concatenate(
        [lax.slice_in_dim(padded, k * dilation, k * dilation + rows, axis=1) for k in order], axis=-1
    )


def local(codes, embed, first_weight_taps, second_weight_taps, cotangent):
    one, two = FIRST_DILATION, SECOND_DILATION
    panel = codes.shape[1]
    reach_hidden = 2 * two
    reach_codes = reach_hidden + one
    channels = cotangent.shape[2]
    codes_row = codes.astype(cotangent.dtype)
    head = jnp.concatenate(
        [cotangent[:, :two], jnp.pad(codes_row[:, :reach_codes], ((0, 0), (0, channels - reach_codes)))[:, None]], axis=1
    )
    tail = jnp.concatenate(
        [cotangent[:, panel - two :], jnp.pad(codes_row[:, panel - reach_codes :], ((0, 0), (0, channels - reach_codes)))[:, None]],
        axis=1,
    )
    count = lax.axis_size("seq")
    from_left = lax.ppermute(tail, "seq", [(i, i + 1) for i in range(count - 1)])
    from_right = lax.ppermute(head, "seq", [(i + 1, i) for i in range(count - 1)])
    cot_left, cot_right = from_left[:, :two], from_right[:, :two]
    code_left = from_left[:, two, :reach_codes].astype(jnp.int32)
    code_right = from_right[:, two, :reach_codes].astype(jnp.int32)
    codes_wide = jnp.concatenate([code_left, codes, code_right], axis=1)
    cot_wide = jnp.concatenate([cot_left, cotangent, cot_right], axis=1)

    first_mirror = mirrored_taps(first_weight_taps)
    second_mirror = mirrored_taps(second_weight_taps)

    onehot = (codes_wide[..., None] == jnp.arange(4, dtype=jnp.int32)).astype(jnp.bfloat16)
    features = product(onehot, embed).astype(jnp.bfloat16)
    rows_codes = panel + 2 * reach_codes
    features = jnp.where(inside_window(rows_codes, reach_codes)[None, :, None], features, jnp.zeros_like(features))

    rows_hidden = panel + 2 * reach_hidden
    first_stack = taps_of(features, one, rows_hidden, (0, 1, 2))
    first_activation = both_strands(first_stack, first_weight_taps, first_mirror)
    hidden = jax.nn.gelu(first_activation).astype(jnp.bfloat16)
    hidden = jnp.where(inside_window(rows_hidden, reach_hidden)[None, :, None], hidden, jnp.zeros_like(hidden))

    rows_two = panel + 2 * two
    second_stack = taps_of(hidden, two, rows_two, (0, 1, 2))
    second_activation = both_strands(second_stack, second_weight_taps, second_mirror)
    gelu_two, back_two = jax.vjp(jax.nn.gelu, second_activation)

    hidden_own = lax.slice_in_dim(hidden, reach_hidden, reach_hidden + panel, axis=1)
    block_out = (hidden_own.astype(jnp.float32) + lax.slice_in_dim(gelu_two, two, two + panel, axis=1)).astype(jnp.bfloat16)

    second_grad_wide = back_two(cot_wide.astype(jnp.float32))[0].astype(jnp.bfloat16)
    grad_stack = taps_of(second_grad_wide, two, panel, (2, 1, 0))
    flat_t = jnp.transpose(second_weight_taps, (0, 2, 1))
    mirror_t = jnp.transpose(second_mirror, (0, 2, 1))
    input_contribution = both_strands(grad_stack, flat_t, mirror_t)
    hidden_gradient = cotangent.astype(jnp.float32) + input_contribution

    first_own = lax.slice_in_dim(first_activation, reach_hidden, reach_hidden + panel, axis=1)
    _, back_one = jax.vjp(jax.nn.gelu, first_own)
    first_grad = back_one(hidden_gradient)[0].astype(jnp.bfloat16)

    second_grad_own = lax.slice_in_dim(second_grad_wide, two, two + panel, axis=1)
    second_weight_gradient = folded_half(hidden, second_grad_own, two, reach_hidden - two)
    first_weight_gradient = folded_half(features, first_grad, one, reach_codes - one)
    second_weight_gradient, first_weight_gradient = unfolded_halves(second_weight_gradient, first_weight_gradient)
    return (block_out, first_weight_gradient, second_weight_gradient)


def solution(mesh):
    in_specs = (P("dp", "seq"), P(), P(), P(), P("dp", "seq", None))
    out_specs = (P("dp", "seq", None), P(), P())
    return jax.shard_map(local, mesh=mesh, in_specs=in_specs, out_specs=out_specs, check_vma=False)
```

```python
import jax
import jax.numpy as jnp
from jax import lax
from jax.sharding import PartitionSpec as P

FIRST_DILATION = 4
SECOND_DILATION = 16


def with_halo(cells, sides, width):
    for axis, dim in sides:
        count = lax.axis_size(axis)
        ends = count - 1
        head = lax.slice_in_dim(cells, 0, width, axis=dim)
        tail = lax.slice_in_dim(cells, cells.shape[dim] - width, cells.shape[dim], axis=dim)
        cells = jnp.concatenate(
            [
                lax.ppermute(tail, axis, [(i, (i + 1) % count) for i in range(ends)]),
                cells,
                lax.ppermute(head, axis, [((i + 1) % count, i) for i in range(ends)]),
            ],
            axis=dim,
        )
    return cells


def pad_rows(value, dilation):
    return with_halo(value, (("seq", 1),), dilation)


def stack_rows(padded, dilation, order):
    count_rows = padded.shape[1] - 2 * dilation
    return jnp.concatenate(
        [padded[:, k * dilation : k * dilation + count_rows] for k in order], axis=-1
    )


def product(stacked, matrix):
    shape_in = stacked.shape
    result = jnp.dot(stacked.reshape(-1, shape_in[-1]), matrix, preferred_element_type=jnp.float32)
    return result.reshape(shape_in[:-1] + (matrix.shape[1],))


def weight_term(stacked, grad):
    channels = grad.shape[-1]
    term = jnp.dot(
        stacked.reshape(-1, 3 * channels).T,
        grad.reshape(-1, channels),
        preferred_element_type=jnp.float32,
    )
    return term.reshape(3, channels, channels)


def layer_forward_pass(value, weight, dilation):
    channels = weight.shape[2]
    stacked = stack_rows(pad_rows(value, dilation), dilation, (0, 1, 2))
    flat = weight.reshape(-1, channels)
    reversed_taps = weight[::-1, ::-1, ::-1].reshape(-1, channels)
    both = product(stacked, jnp.concatenate([flat, reversed_taps], axis=1))
    return (both[..., :channels] + both[..., channels:], stacked)


def input_backward_pass(grad, weight, dilation):
    channels = weight.shape[2]
    stacked = stack_rows(pad_rows(grad, dilation), dilation, (2, 1, 0))
    flat_t = jnp.transpose(weight, (0, 2, 1)).reshape(-1, channels)
    reversed_t = jnp.transpose(weight[::-1, ::-1, ::-1], (0, 2, 1)).reshape(-1, channels)
    both = product(stacked, jnp.concatenate([flat_t, reversed_t], axis=1))
    return both[..., :channels] + both[..., channels:]


def strand_total(stacked, grad):
    term = weight_term(stacked, grad)
    return term + term[::-1, ::-1, ::-1]


def exchange_groups():
    groups = []
    for axis, shift, radix in (("dp", 0, 4), ("seq", 2, 4), ("dp", 2, 4), ("seq", 0, 2), ("seq", 1, 2)):
        if (radix << shift) <= lax.axis_size(axis):
            groups.append((axis, shift, radix))
    return groups


def partner_pairs(axis, shift, offset):
    count = lax.axis_size(axis)
    return [(i, i ^ (offset << shift)) for i in range(count)]


def butterfly_sum(rows, scattered=2):
    kept = []
    groups = exchange_groups()
    for axis, shift, radix in groups[:scattered]:
        place = (lax.axis_index(axis) >> shift) & (radix - 1)
        width = rows.shape[0] // radix
        total = lax.dynamic_slice_in_dim(rows, place * width, width)
        for offset in range(1, radix):
            sent = lax.dynamic_slice_in_dim(rows, (place ^ offset) * width, width)
            total = total + lax.ppermute(sent, axis, partner_pairs(axis, shift, offset))
        rows = total
        kept.append((axis, shift, radix, place))
    for axis, shift, radix in groups[scattered:]:
        place = (lax.axis_index(axis) >> shift) & (radix - 1)
        pieces = [rows] + [lax.ppermute(rows, axis, partner_pairs(axis, shift, offset)) for offset in range(1, radix)]
        total = None
        for position in range(radix):
            chosen = pieces[0]
            for offset in range(1, radix):
                chosen = jnp.where((position ^ place) == offset, pieces[offset], chosen)
            total = chosen if total is None else total + chosen
        rows = total
    for axis, shift, radix, place in reversed(kept):
        width = rows.shape[0]
        pieces = [rows] + [lax.ppermute(rows, axis, partner_pairs(axis, shift, offset)) for offset in range(1, radix)]
        order = jnp.arange(radix, dtype=jnp.int32) ^ place
        rows = jnp.take(jnp.stack(pieces), order, axis=0).reshape((width * radix,) + rows.shape[1:])
    return rows


def reversed_channels(value, keep=None):
    anti = anti_diagonal(value.shape[-1])
    if keep is not None:
        anti = anti[:, :keep]
    return jnp.einsum("btc,cd->btd", value, anti, preferred_element_type=jnp.float32).astype(value.dtype)


def folded_half(value, grad, dilation, offset):
    channels = grad.shape[-1]
    half = channels // 2
    panel = grad.shape[1]
    mirror = reversed_channels(value)
    grad_left = grad[0, :, :half]
    grad_mirror = reversed_channels(grad, half)[0]
    blocks = []
    for k in range(3):
        own = lax.slice_in_dim(value, offset + k * dilation, offset + k * dilation + panel, axis=1)[0]
        other = lax.slice_in_dim(mirror, offset + (2 - k) * dilation, offset + (2 - k) * dilation + panel, axis=1)[0]
        blocks.append(
            jnp.dot(grad_left.T, own, preferred_element_type=jnp.float32)
            + jnp.dot(grad_mirror.T, other, preferred_element_type=jnp.float32)
        )
    return jnp.concatenate(blocks, axis=0)


def unfolded_halves(first, second):
    rows, channels = first.shape
    half = rows // 3
    total = butterfly_sum(jnp.concatenate([first, second], axis=0))
    outs = []
    for i in range(2):
        part = total[i * rows : (i + 1) * rows]
        taps = [part[k * half : (k + 1) * half].T for k in range(3)]
        outs.append(jnp.stack([jnp.concatenate([taps[k], taps[2 - k][::-1, ::-1]], axis=1) for k in range(3)]))
    return outs


def folded_term(stacked, grad):
    channels = grad.shape[-1]
    term = jnp.dot(
        grad.reshape(-1, channels).T,
        stacked.reshape(-1, 3 * channels),
        preferred_element_type=jnp.float32,
    )
    half = channels // 2
    return term[:half] + term[half:][::-1, ::-1]


def unfolded_sums(first, second):
    half, width = first.shape
    lanes = width // 3
    rows = half * 3
    total = butterfly_sum(jnp.concatenate([first.reshape(rows, lanes), second.reshape(rows, lanes)], axis=0))
    outs = []
    for i in range(2):
        part = total[i * rows : (i + 1) * rows].reshape(half, width)
        full = jnp.concatenate([part, part[::-1, ::-1]], axis=0)
        outs.append(jnp.transpose(full.reshape(2 * half, 3, width // 3), (1, 2, 0)))
    return outs


def symmetric_sum(first, second):
    shape = first.shape
    flat_rows = shape[0] * shape[1]
    half = flat_rows // 2
    halves = [g.reshape(flat_rows, shape[2])[:half] for g in (first, second)]
    total = butterfly_sum(jnp.concatenate(halves, axis=0))
    outs = []
    for i in range(2):
        part = total[i * half : (i + 1) * half]
        outs.append(jnp.concatenate([part, part[::-1, ::-1]], axis=0).reshape(shape))
    return outs


def neighbour_halo(cells, width, dim):
    count = lax.axis_size("seq")
    head = lax.slice_in_dim(cells, 0, width, axis=dim)
    tail = lax.slice_in_dim(cells, cells.shape[dim] - width, cells.shape[dim], axis=dim)
    from_left = lax.ppermute(tail, "seq", [(i, i + 1) for i in range(count - 1)])
    from_right = lax.ppermute(head, "seq", [(i + 1, i) for i in range(count - 1)])
    return from_left, from_right


def inside_window(rows, reach):
    panel = rows - 2 * reach
    place = lax.axis_index("seq") * panel + jnp.arange(rows, dtype=jnp.int32) - reach
    return (place >= 0) & (place < lax.axis_size("seq") * panel)


def anti_diagonal(channels):
    i = jnp.arange(channels, dtype=jnp.int32)
    return (i[:, None] + i[None, :] == channels - 1).astype(jnp.bfloat16)


def mirrored_taps(weight):
    anti = anti_diagonal(weight.shape[1])
    flipped = weight[::-1]
    left = jnp.einsum("ab,kbc->kac", anti, flipped, preferred_element_type=jnp.float32).astype(weight.dtype)
    return jnp.einsum("kab,bc->kac", left, anti, preferred_element_type=jnp.float32).astype(weight.dtype)


def both_strands(stacked, matrix, mirrored):
    channels = matrix.shape[2]
    both = product(stacked, jnp.concatenate([matrix.reshape(-1, channels), mirrored.reshape(-1, channels)], axis=1))
    return both[..., :channels] + both[..., channels:]


def taps_of(padded, dilation, rows, order):
    return jnp.concatenate(
        [lax.slice_in_dim(padded, k * dilation, k * dilation + rows, axis=1) for k in order], axis=-1
    )


def local(codes, embed, first_weight_taps, second_weight_taps, cotangent):
    one, two = FIRST_DILATION, SECOND_DILATION
    panel = codes.shape[1]
    reach_hidden = 2 * two
    reach_codes = reach_hidden + one
    channels = cotangent.shape[2]
    codes_row = codes.astype(cotangent.dtype)
    head = jnp.concatenate(
        [cotangent[:, :two], jnp.pad(codes_row[:, :reach_codes], ((0, 0), (0, channels - reach_codes)))[:, None]], axis=1
    )
    tail = jnp.concatenate(
        [cotangent[:, panel - two :], jnp.pad(codes_row[:, panel - reach_codes :], ((0, 0), (0, channels - reach_codes)))[:, None]],
        axis=1,
    )
    count = lax.axis_size("seq")
    from_left = lax.ppermute(tail, "seq", [(i, i + 1) for i in range(count - 1)])
    from_right = lax.ppermute(head, "seq", [(i + 1, i) for i in range(count - 1)])
    cot_left, cot_right = from_left[:, :two], from_right[:, :two]
    code_left = from_left[:, two, :reach_codes].astype(jnp.int32)
    code_right = from_right[:, two, :reach_codes].astype(jnp.int32)
    codes_wide = jnp.concatenate([code_left, codes, code_right], axis=1)
    cot_wide = jnp.concatenate([cot_left, cotangent, cot_right], axis=1)

    first_mirror = mirrored_taps(first_weight_taps)
    second_mirror = mirrored_taps(second_weight_taps)

    onehot = (codes_wide[..., None] == jnp.arange(4, dtype=jnp.int32)).astype(jnp.bfloat16)
    features = product(onehot, embed).astype(jnp.bfloat16)
    rows_codes = panel + 2 * reach_codes
    features = jnp.where(inside_window(rows_codes, reach_codes)[None, :, None], features, jnp.zeros_like(features))

    rows_hidden = panel + 2 * reach_hidden
    first_stack = taps_of(features, one, rows_hidden, (0, 1, 2))
    first_activation = both_strands(first_stack, first_weight_taps, first_mirror)
    hidden = jax.nn.gelu(first_activation).astype(jnp.bfloat16)
    hidden = jnp.where(inside_window(rows_hidden, reach_hidden)[None, :, None], hidden, jnp.zeros_like(hidden))

    rows_two = panel + 2 * two
    second_stack = taps_of(hidden, two, rows_two, (0, 1, 2))
    second_activation = both_strands(second_stack, second_weight_taps, second_mirror)
    gelu_two, back_two = jax.vjp(jax.nn.gelu, second_activation)

    hidden_own = lax.slice_in_dim(hidden, reach_hidden, reach_hidden + panel, axis=1)
    block_out = (hidden_own.astype(jnp.float32) + lax.slice_in_dim(gelu_two, two, two + panel, axis=1)).astype(jnp.bfloat16)

    second_grad_wide = back_two(cot_wide.astype(jnp.float32))[0].astype(jnp.bfloat16)
    grad_stack = taps_of(second_grad_wide, two, panel, (2, 1, 0))
    flat_t = jnp.transpose(second_weight_taps, (0, 2, 1))
    mirror_t = jnp.transpose(second_mirror, (0, 2, 1))
    input_contribution = both_strands(grad_stack, flat_t, mirror_t)
    hidden_gradient = cotangent.astype(jnp.float32) + input_contribution

    first_own = lax.slice_in_dim(first_activation, reach_hidden, reach_hidden + panel, axis=1)
    _, back_one = jax.vjp(jax.nn.gelu, first_own)
    first_grad = back_one(hidden_gradient)[0].astype(jnp.bfloat16)

    second_grad_own = lax.slice_in_dim(second_grad_wide, two, two + panel, axis=1)
    second_weight_gradient = folded_half(hidden, second_grad_own, two, reach_hidden - two)
    first_weight_gradient = folded_half(features, first_grad, one, reach_codes - one)
    second_weight_gradient, first_weight_gradient = unfolded_halves(second_weight_gradient, first_weight_gradient)
    return (block_out, first_weight_gradient, second_weight_gradient)


def solution(mesh):
    in_specs = (P("dp", "seq"), P(), P(), P(), P("dp", "seq", None))
    out_specs = (P("dp", "seq", None), P(), P())
    return jax.shard_map(local, mesh=mesh, in_specs=in_specs, out_specs=out_specs, check_vma=False)
```

```python
import jax
import jax.numpy as jnp
from jax import lax
from jax.sharding import PartitionSpec as P

FIRST_DILATION = 4
SECOND_DILATION = 16


def with_halo(cells, sides, width):
    for axis, dim in sides:
        count = lax.axis_size(axis)
        ends = count - 1
        head = lax.slice_in_dim(cells, 0, width, axis=dim)
        tail = lax.slice_in_dim(cells, cells.shape[dim] - width, cells.shape[dim], axis=dim)
        cells = jnp.concatenate(
            [
                lax.ppermute(tail, axis, [(i, (i + 1) % count) for i in range(ends)]),
                cells,
                lax.ppermute(head, axis, [((i + 1) % count, i) for i in range(ends)]),
            ],
            axis=dim,
        )
    return cells


def pad_rows(value, dilation):
    return with_halo(value, (("seq", 1),), dilation)


def stack_rows(padded, dilation, order):
    count_rows = padded.shape[1] - 2 * dilation
    return jnp.concatenate(
        [padded[:, k * dilation : k * dilation + count_rows] for k in order], axis=-1
    )


def product(stacked, matrix):
    shape_in = stacked.shape
    result = jnp.dot(stacked.reshape(-1, shape_in[-1]), matrix, preferred_element_type=jnp.float32)
    return result.reshape(shape_in[:-1] + (matrix.shape[1],))


def weight_term(stacked, grad):
    channels = grad.shape[-1]
    term = jnp.dot(
        stacked.reshape(-1, 3 * channels).T,
        grad.reshape(-1, channels),
        preferred_element_type=jnp.float32,
    )
    return term.reshape(3, channels, channels)


def layer_forward_pass(value, weight, dilation):
    channels = weight.shape[2]
    stacked = stack_rows(pad_rows(value, dilation), dilation, (0, 1, 2))
    flat = weight.reshape(-1, channels)
    reversed_taps = weight[::-1, ::-1, ::-1].reshape(-1, channels)
    both = product(stacked, jnp.concatenate([flat, reversed_taps], axis=1))
    return (both[..., :channels] + both[..., channels:], stacked)


def input_backward_pass(grad, weight, dilation):
    channels = weight.shape[2]
    stacked = stack_rows(pad_rows(grad, dilation), dilation, (2, 1, 0))
    flat_t = jnp.transpose(weight, (0, 2, 1)).reshape(-1, channels)
    reversed_t = jnp.transpose(weight[::-1, ::-1, ::-1], (0, 2, 1)).reshape(-1, channels)
    both = product(stacked, jnp.concatenate([flat_t, reversed_t], axis=1))
    return both[..., :channels] + both[..., channels:]


def strand_total(stacked, grad):
    term = weight_term(stacked, grad)
    return term + term[::-1, ::-1, ::-1]


def exchange_groups():
    groups = []
    for axis, shift, radix in (("dp", 0, 4), ("seq", 2, 4), ("dp", 2, 4), ("seq", 0, 2), ("seq", 1, 2)):
        if (radix << shift) <= lax.axis_size(axis):
            groups.append((axis, shift, radix))
    return groups


def partner_pairs(axis, shift, offset):
    count = lax.axis_size(axis)
    return [(i, i ^ (offset << shift)) for i in range(count)]


def butterfly_sum(rows, scattered=2):
    kept = []
    groups = exchange_groups()
    for axis, shift, radix in groups[:scattered]:
        place = (lax.axis_index(axis) >> shift) & (radix - 1)
        width = rows.shape[0] // radix
        quarters = [rows[q * width : (q + 1) * width] for q in range(radix)]

        def pick(index, choices=quarters):
            chosen = choices[0]
            for q in range(1, radix):
                chosen = jnp.where(index == q, choices[q], chosen)
            return chosen

        total = pick(place)
        for offset in range(1, radix):
            sent = pick(place ^ offset)
            total = total + lax.ppermute(sent, axis, partner_pairs(axis, shift, offset))
        rows = total
        kept.append((axis, shift, radix, place))
    for axis, shift, radix in groups[scattered:]:
        place = (lax.axis_index(axis) >> shift) & (radix - 1)
        pieces = [rows] + [lax.ppermute(rows, axis, partner_pairs(axis, shift, offset)) for offset in range(1, radix)]
        total = None
        for position in range(radix):
            chosen = pieces[0]
            for offset in range(1, radix):
                chosen = jnp.where((position ^ place) == offset, pieces[offset], chosen)
            total = chosen if total is None else total + chosen
        rows = total
    for axis, shift, radix, place in reversed(kept):
        width = rows.shape[0]
        pieces = [rows] + [lax.ppermute(rows, axis, partner_pairs(axis, shift, offset)) for offset in range(1, radix)]
        slots = []
        for position in range(radix):
            chosen = pieces[0]
            for offset in range(1, radix):
                chosen = jnp.where((position ^ place) == offset, pieces[offset], chosen)
            slots.append(chosen)
        rows = jnp.concatenate(slots, axis=0)
    return rows


def reversed_channels(value, keep=None):
    anti = anti_diagonal(value.shape[-1])
    if keep is not None:
        anti = anti[:, :keep]
    return jnp.einsum("btc,cd->btd", value, anti, preferred_element_type=jnp.float32).astype(value.dtype)


def folded_half(value, grad, dilation, offset):
    channels = grad.shape[-1]
    half = channels // 2
    panel = grad.shape[1]
    mirror = reversed_channels(value)
    grad_left = grad[0, :, :half]
    grad_mirror = reversed_channels(grad, half)[0]
    blocks = []
    for k in range(3):
        own = lax.slice_in_dim(value, offset + k * dilation, offset + k * dilation + panel, axis=1)[0]
        other = lax.slice_in_dim(mirror, offset + (2 - k) * dilation, offset + (2 - k) * dilation + panel, axis=1)[0]
        blocks.append(
            jnp.dot(grad_left.T, own, preferred_element_type=jnp.float32)
            + jnp.dot(grad_mirror.T, other, preferred_element_type=jnp.float32)
        )
    return jnp.concatenate(blocks, axis=0)


def unfolded_halves(first, second):
    rows, channels = first.shape
    half = rows // 3
    total = butterfly_sum(jnp.concatenate([first, second], axis=0))
    outs = []
    for i in range(2):
        part = total[i * rows : (i + 1) * rows]
        taps = [part[k * half : (k + 1) * half].T for k in range(3)]
        outs.append(jnp.stack([jnp.concatenate([taps[k], taps[2 - k][::-1, ::-1]], axis=1) for k in range(3)]))
    return outs


def folded_term(stacked, grad):
    channels = grad.shape[-1]
    term = jnp.dot(
        grad.reshape(-1, channels).T,
        stacked.reshape(-1, 3 * channels),
        preferred_element_type=jnp.float32,
    )
    half = channels // 2
    return term[:half] + term[half:][::-1, ::-1]


def unfolded_sums(first, second):
    half, width = first.shape
    lanes = width // 3
    rows = half * 3
    total = butterfly_sum(jnp.concatenate([first.reshape(rows, lanes), second.reshape(rows, lanes)], axis=0))
    outs = []
    for i in range(2):
        part = total[i * rows : (i + 1) * rows].reshape(half, width)
        full = jnp.concatenate([part, part[::-1, ::-1]], axis=0)
        outs.append(jnp.transpose(full.reshape(2 * half, 3, width // 3), (1, 2, 0)))
    return outs


def symmetric_sum(first, second):
    shape = first.shape
    flat_rows = shape[0] * shape[1]
    half = flat_rows // 2
    halves = [g.reshape(flat_rows, shape[2])[:half] for g in (first, second)]
    total = butterfly_sum(jnp.concatenate(halves, axis=0))
    outs = []
    for i in range(2):
        part = total[i * half : (i + 1) * half]
        outs.append(jnp.concatenate([part, part[::-1, ::-1]], axis=0).reshape(shape))
    return outs


def neighbour_halo(cells, width, dim):
    count = lax.axis_size("seq")
    head = lax.slice_in_dim(cells, 0, width, axis=dim)
    tail = lax.slice_in_dim(cells, cells.shape[dim] - width, cells.shape[dim], axis=dim)
    from_left = lax.ppermute(tail, "seq", [(i, i + 1) for i in range(count - 1)])
    from_right = lax.ppermute(head, "seq", [(i + 1, i) for i in range(count - 1)])
    return from_left, from_right


def inside_window(rows, reach):
    panel = rows - 2 * reach
    place = lax.axis_index("seq") * panel + jnp.arange(rows, dtype=jnp.int32) - reach
    return (place >= 0) & (place < lax.axis_size("seq") * panel)


def anti_diagonal(channels):
    i = jnp.arange(channels, dtype=jnp.int32)
    return (i[:, None] + i[None, :] == channels - 1).astype(jnp.bfloat16)


def mirrored_taps(weight):
    anti = anti_diagonal(weight.shape[1])
    flipped = weight[::-1]
    left = jnp.einsum("ab,kbc->kac", anti, flipped, preferred_element_type=jnp.float32).astype(weight.dtype)
    return jnp.einsum("kab,bc->kac", left, anti, preferred_element_type=jnp.float32).astype(weight.dtype)


def both_strands(stacked, matrix, mirrored):
    channels = matrix.shape[2]
    both = product(stacked, jnp.concatenate([matrix.reshape(-1, channels), mirrored.reshape(-1, channels)], axis=1))
    return both[..., :channels] + both[..., channels:]


def taps_of(padded, dilation, rows, order):
    return jnp.concatenate(
        [lax.slice_in_dim(padded, k * dilation, k * dilation + rows, axis=1) for k in order], axis=-1
    )


def local(codes, embed, first_weight_taps, second_weight_taps, cotangent):
    one, two = FIRST_DILATION, SECOND_DILATION
    panel = codes.shape[1]
    reach_hidden = 2 * two
    reach_codes = reach_hidden + one
    channels = cotangent.shape[2]
    codes_row = codes.astype(cotangent.dtype)
    head = jnp.concatenate(
        [cotangent[:, :two], jnp.pad(codes_row[:, :reach_codes], ((0, 0), (0, channels - reach_codes)))[:, None]], axis=1
    )
    tail = jnp.concatenate(
        [cotangent[:, panel - two :], jnp.pad(codes_row[:, panel - reach_codes :], ((0, 0), (0, channels - reach_codes)))[:, None]],
        axis=1,
    )
    count = lax.axis_size("seq")
    from_left = lax.ppermute(tail, "seq", [(i, i + 1) for i in range(count - 1)])
    from_right = lax.ppermute(head, "seq", [(i + 1, i) for i in range(count - 1)])
    cot_left, cot_right = from_left[:, :two], from_right[:, :two]
    code_left = from_left[:, two, :reach_codes].astype(jnp.int32)
    code_right = from_right[:, two, :reach_codes].astype(jnp.int32)
    codes_wide = jnp.concatenate([code_left, codes, code_right], axis=1)
    cot_wide = jnp.concatenate([cot_left, cotangent, cot_right], axis=1)

    first_mirror = mirrored_taps(first_weight_taps)
    second_mirror = mirrored_taps(second_weight_taps)

    onehot = (codes_wide[..., None] == jnp.arange(4, dtype=jnp.int32)).astype(jnp.bfloat16)
    features = product(onehot, embed).astype(jnp.bfloat16)
    rows_codes = panel + 2 * reach_codes
    features = jnp.where(inside_window(rows_codes, reach_codes)[None, :, None], features, jnp.zeros_like(features))

    rows_hidden = panel + 2 * reach_hidden
    first_stack = taps_of(features, one, rows_hidden, (0, 1, 2))
    first_activation = both_strands(first_stack, first_weight_taps, first_mirror)
    hidden = jax.nn.gelu(first_activation).astype(jnp.bfloat16)
    hidden = jnp.where(inside_window(rows_hidden, reach_hidden)[None, :, None], hidden, jnp.zeros_like(hidden))

    rows_two = panel + 2 * two
    second_stack = taps_of(hidden, two, rows_two, (0, 1, 2))
    second_activation = both_strands(second_stack, second_weight_taps, second_mirror)
    gelu_two, back_two = jax.vjp(jax.nn.gelu, second_activation)

    hidden_own = lax.slice_in_dim(hidden, reach_hidden, reach_hidden + panel, axis=1)
    block_out = (hidden_own.astype(jnp.float32) + lax.slice_in_dim(gelu_two, two, two + panel, axis=1)).astype(jnp.bfloat16)

    second_grad_wide = back_two(cot_wide.astype(jnp.float32))[0].astype(jnp.bfloat16)
    grad_stack = taps_of(second_grad_wide, two, panel, (2, 1, 0))
    flat_t = jnp.transpose(second_weight_taps, (0, 2, 1))
    mirror_t = jnp.transpose(second_mirror, (0, 2, 1))
    input_contribution = both_strands(grad_stack, flat_t, mirror_t)
    hidden_gradient = cotangent.astype(jnp.float32) + input_contribution

    first_own = lax.slice_in_dim(first_activation, reach_hidden, reach_hidden + panel, axis=1)
    _, back_one = jax.vjp(jax.nn.gelu, first_own)
    first_grad = back_one(hidden_gradient)[0].astype(jnp.bfloat16)

    second_grad_own = lax.slice_in_dim(second_grad_wide, two, two + panel, axis=1)
    second_weight_gradient = folded_half(hidden, second_grad_own, two, reach_hidden - two)
    first_weight_gradient = folded_half(features, first_grad, one, reach_codes - one)
    second_weight_gradient, first_weight_gradient = unfolded_halves(second_weight_gradient, first_weight_gradient)
    return (block_out, first_weight_gradient, second_weight_gradient)


def solution(mesh):
    in_specs = (P("dp", "seq"), P(), P(), P(), P("dp", "seq", None))
    out_specs = (P("dp", "seq", None), P(), P())
    return jax.shard_map(local, mesh=mesh, in_specs=in_specs, out_specs=out_specs, check_vma=False)
```
